256 devices in a mesh: seq: 64 (over x, z, core), head: 4 (over y).
Axes of the slice: x: 4, y: 4, z: 8, core: 2. Of those that a mesh axis runs over, the one named last changes fastest.
Arguments:
- query_rows: bfloat16 [65536, 4, 128], P(('seq', 'head')), may hold values from -5 to 5
- key_rows: bfloat16 [65536, 4, 128], P(('seq', 'head')), may hold values from -5 to 5
- value_rows: bfloat16 [65536, 4, 128], P(('seq', 'head')), may hold values from -6 to 6
- grad_rows: bfloat16 [65536, 4, 128], P(('seq', 'head')), may hold values from -6 to 6
- assignment: int32 [65536, 4], P(('seq', 'head')), may hold values from 0 to 63, as said below
- position: int32 [65536, 4], P(('seq', 'head')), may hold values from 0 to 1023, as said below
Outputs:
- attended: bfloat16 [65536, 4, 128], P(('seq', 'head'))
- grad_query: bfloat16 [65536, 4, 128], P(('seq', 'head'))
- grad_key: bfloat16 [65536, 4, 128], P(('seq', 'head'))
- grad_value: bfloat16 [65536, 4, 128], P(('seq', 'head'))
The draws below stay inside these ranges and needn't reach their ends.
Inputs may be any that keep to these rules, and one draw needn't show every extreme that they name: `assignment`: in each head every cluster holds exactly 1024 tokens. The 256 tokens of one device send at most 6 tokens of one head to one cluster, and exactly 6 for some device, head and cluster in every draw. `position`: within each head and cluster the 1024 tokens have the places 0 to 1023, each once.
All inputs are finite; a program needn't handle non-finite values.
Results may differ from the reference program's by a relative error of at most 0.025.
Values may be sent and summed in bfloat16 or wider, within the bound.
No kernel may reach another device: no remote copies, remote signals or barrier semaphores. Data moves between devices by JAX's collectives and lax.ppermute only.
A program may use at most 64 MiB of HBM per device.

```python
import math
import jax
import jax.numpy as jnp
from jax import lax

HEAD_DIM = 128
TOK_DEV = 1024
HEADS = 4
CLUSTERS = 64
TOKENS = 65536
ROWS_DEV = 256


def count_table(key):
    table_rows = TOKENS // ROWS_DEV
    mean_count = ROWS_DEV // CLUSTERS
    half_count = mean_count // 2
    top_value = mean_count + half_count
    shuffled = jax.random.permutation(jax.random.fold_in(key, 1), CLUSTERS)
    row_ids = jnp.arange(table_rows, dtype=jnp.int32)
    col_ids = jnp.arange(CLUSTERS, dtype=jnp.int32)
    raised = shuffled[row_ids % CLUSTERS]
    lowered = shuffled[(row_ids + 1) % CLUSTERS]
    table = mean_count + half_count * ((col_ids[None, :] == raised[:, None]).astype(jnp.int32) - (col_ids[None, :] == lowered[:, None]).astype(jnp.int32))

    def one_move(turn, current):
        move_keys = jax.random.split(jax.random.fold_in(key, 1000 + turn), 5)
        row_one = jax.random.randint(move_keys[0], (), 0, table_rows)
        row_two = (row_one + jax.random.randint(move_keys[1], (), 1, table_rows)) % table_rows
        col_one = jax.random.randint(move_keys[2], (), 0, CLUSTERS)
        col_two = (col_one + jax.random.randint(move_keys[3], (), 1, CLUSTERS)) % CLUSTERS
        amount = jax.random.randint(move_keys[4], (), 1, half_count + 1)
        first = current[row_one, col_one]
        second = current[row_two, col_two]
        cross_one = current[row_one, col_two]
        cross_two = current[row_two, col_one]
        valid = (first >= 1) & (first + amount <= top_value - 1) & (second >= 1) & (second + amount <= top_value - 1)
        valid = valid & (cross_one - amount >= 0) & (cross_one <= top_value - 1) & (cross_two - amount >= 0) & (cross_two <= top_value - 1)
        step_size = jnp.where(valid, amount, 0)
        current = current.at[row_one, col_one].add(step_size)
        current = current.at[row_two, col_two].add(step_size)
        current = current.at[row_one, col_two].add(-step_size)
        current = current.at[row_two, col_one].add(-step_size)
        return current
    return lax.fori_loop(0, 2 * table_rows * CLUSTERS, one_move, table)


def routing(key):
    base_key = jax.random.fold_in(key, 4242)
    table_rows = TOKENS // ROWS_DEV

    def one_head(head_index):
        head_key = jax.random.fold_in(base_key, head_index)
        table = count_table(head_key)
        bounds = jnp.cumsum(table, axis=1)
        slot_ids = jnp.arange(ROWS_DEV, dtype=jnp.int32)
        listed = jnp.sum((bounds[:, None, :] <= slot_ids[None, :, None]).astype(jnp.int32), axis=2)
        shuffles = jax.vmap(lambda sub_key: jax.random.permutation(sub_key, ROWS_DEV))(jax.random.split(jax.random.fold_in(head_key, 2), table_rows))
        assigned = jnp.take_along_axis(listed, shuffles, axis=1).reshape(TOKENS)
        ranking = jax.random.permutation(jax.random.fold_in(head_key, 3), TOKENS)
        sorted_order = jnp.argsort(assigned * TOKENS + ranking, stable=True)
        placed = jnp.zeros((TOKENS,), jnp.int32).at[sorted_order].set(jnp.arange(TOKENS, dtype=jnp.int32) % TOK_DEV)
        return (assigned, placed)
    assigned_all, placed_all = jax.vmap(one_head)(jnp.arange(HEADS, dtype=jnp.int32))
    return (assigned_all.T.astype(jnp.int32), placed_all.T.astype(jnp.int32))


def draw_query_rows(key, part):
    drawn = jnp.clip(jax.random.normal(jax.random.fold_in(key, 11), (TOKENS, HEADS, HEAD_DIM), jnp.float32), -4.0, 4.0)
    return drawn.astype(jnp.bfloat16)


def draw_key_rows(key, part):
    drawn = jnp.clip(jax.random.normal(jax.random.fold_in(key, 12), (TOKENS, HEADS, HEAD_DIM), jnp.float32), -4.0, 4.0)
    return drawn.astype(jnp.bfloat16)


def draw_assignment(key, part):
    return routing(key)[0]


def draw_position(key, part):
    return routing(key)[1]


def levels(key, shape, cuts, low, high):
    def one(axis_at, shards_of):
        heights = jax.random.uniform(jax.random.fold_in(jax.random.fold_in(key, 6), axis_at), (shards_of,), jnp.float32, low / len(cuts), high / len(cuts))
        return jnp.repeat(jnp.exp(heights), shape[axis_at] // shards_of).reshape((-1,) + (1,) * (len(shape) - axis_at - 1))

    factor_of = one(*cuts[0])
    for cut in cuts[1:]:
        factor_of = factor_of * one(*cut)
    return factor_of


def scatter_about(key, extent, width, most, cuts=(), kind=jnp.bfloat16):
    result = width * jax.random.normal(key, extent, jnp.float32)
    if cuts:
        result = result * levels(key, extent, cuts, -0.22, 0.18)
    return jnp.clip(result, -most, most).astype(kind)


def setup_inputs(seed: int = 0) -> dict:
    streams_of = jax.random.split(jax.random.key(seed), 7)
    return {
        "query_rows": draw_query_rows(jax.random.fold_in(streams_of[6], 71), 0),
        "key_rows": draw_key_rows(jax.random.fold_in(streams_of[6], 71), 0),
        "value_rows": scatter_about(streams_of[2], (TOKENS, HEADS, HEAD_DIM), 1.0, 6.0, ((0, 256),)),
        "grad_rows": scatter_about(streams_of[3], (TOKENS, HEADS, HEAD_DIM), 1.0, 6.0, ((0, 256),)),
        "assignment": draw_assignment(jax.random.fold_in(streams_of[6], 71), 0),
        "position": draw_position(jax.random.fold_in(streams_of[6], 71), 0),
    }


def one_cluster(pieces):
    query_block, key_block, value_block, grad_block = pieces
    row_count = query_block.shape[0]
    score_scale = 1.0 / math.sqrt(query_block.shape[1])
    row_ids = jnp.arange(row_count, dtype=jnp.int32)
    allowed = row_ids[None, :] <= row_ids[:, None]
    scores = jnp.dot(query_block, key_block.T, preferred_element_type=jnp.float32) * score_scale
    scores = jnp.where(allowed, scores, -jnp.inf)
    row_top = lax.optimization_barrier(jnp.max(scores, axis=1, keepdims=True))
    weights = jnp.exp(scores - row_top)
    probabilities = weights / lax.optimization_barrier(jnp.sum(weights, axis=1, keepdims=True))
    probs_low = probabilities.astype(jnp.bfloat16)
    attended_block = jnp.dot(probs_low, value_block, preferred_element_type=jnp.float32).astype(jnp.bfloat16)
    grad_prob = jnp.dot(grad_block, value_block.T, preferred_element_type=jnp.float32)
    row_delta = lax.optimization_barrier(jnp.sum(grad_block.astype(jnp.float32) * attended_block.astype(jnp.float32), axis=1, keepdims=True))
    grad_score = (probabilities * (grad_prob - row_delta)).astype(jnp.bfloat16)
    grad_query_block = (jnp.dot(grad_score, key_block, preferred_element_type=jnp.float32) * score_scale).astype(jnp.bfloat16)
    grad_key_block = (jnp.dot(grad_score.T, query_block, preferred_element_type=jnp.float32) * score_scale).astype(jnp.bfloat16)
    grad_value_block = jnp.dot(probs_low.T, grad_block, preferred_element_type=jnp.float32).astype(jnp.bfloat16)
    return (attended_block, grad_query_block, grad_key_block, grad_value_block)

def reference(query_rows, key_rows, value_rows, grad_rows, assignment, position):
    token_count = query_rows.shape[0]
    slot_place = assignment * TOK_DEV + position
    token_ids = jnp.arange(token_count, dtype=jnp.int32)
    collected = [[], [], [], []]
    for head_index in range(HEADS):
        slot_column = slot_place[:, head_index].astype(jnp.int32)
        slot_owner = jnp.zeros((token_count,), jnp.int32).at[slot_column].set(token_ids)
        pieces = tuple((source[slot_owner, head_index].reshape(CLUSTERS, TOK_DEV, source.shape[2]) for source in (query_rows, key_rows, value_rows, grad_rows)))
        results = lax.map(one_cluster, pieces)
        for member in range(4):
            collected[member].append(results[member].reshape(token_count, -1)[slot_column])
    return (jnp.stack(collected[0], axis=1), jnp.stack(collected[1], axis=1), jnp.stack(collected[2], axis=1), jnp.stack(collected[3], axis=1))
```

```python
import math

import jax
import jax.numpy as jnp
from jax import lax
from jax.sharding import PartitionSpec as P


def split_up(x, dim, devices):
    dims = x.shape
    parts = x.reshape(*dims[:dim], devices, dims[dim] // devices, *dims[dim + 1 :])
    return jnp.moveaxis(parts, dim, 0)


def in_order(parts, dim):
    dims = list(parts.shape[1:])
    dims[dim] *= parts.shape[0]
    return jnp.moveaxis(parts, 0, dim).reshape(dims)


def joined_exchange(x, axis, axes, splits, concats):
    sizes = [lax.axis_size(a) for a in axes]
    parts = split_up(x, splits[0], sizes[0])
    parts = jnp.moveaxis(split_up(parts, splits[1] + 1, sizes[1]), 0, 1)
    inside = parts.shape[2:]
    parts = parts.reshape(-1, *inside)
    parts = lax.all_to_all(parts, axis, split_axis=0, concat_axis=0, tiled=True)
    parts = in_order(parts.reshape(*sizes, *inside), concats[0] + 1)
    return in_order(parts, concats[1])


def cluster_slots(assign_cols, clusters, capacity):
    row_count, group_count = assign_cols.shape
    hits = assign_cols[:, :, None] == jnp.arange(clusters, dtype=jnp.int32)[None, None, :]
    onehot = hits.astype(jnp.bfloat16).reshape(row_count, group_count * clusters)
    lower = (
        lax.broadcasted_iota(jnp.int32, (row_count, row_count), 1)
        < lax.broadcasted_iota(jnp.int32, (row_count, row_count), 0)
    ).astype(jnp.bfloat16)
    earlier = jnp.dot(lower, onehot, preferred_element_type=jnp.float32).reshape(
        row_count, group_count, clusters
    )
    within = jnp.sum(jnp.where(hits, earlier, 0.0), axis=2).astype(jnp.int32)
    return assign_cols * capacity + within


def pack_slots(group_rows, group_slot, group_place, slot_count, empty_place):
    slot_ids = jnp.arange(slot_count, dtype=jnp.int32)
    hits = slot_ids[None, :, None] == group_slot[:, None, :]
    packed = jnp.einsum(
        "gsr,grf->gsf", hits.astype(jnp.bfloat16), group_rows, preferred_element_type=jnp.float32
    ).astype(jnp.bfloat16)
    filled = jnp.any(hits, axis=2)
    places = jnp.where(
        filled, jnp.sum(jnp.where(hits, group_place[:, None, :], 0), axis=2), empty_place
    )
    return (packed, places)


def place_tables(flat_place, cluster_len, block_rows):
    tables = []
    for block_index in range(cluster_len // block_rows):
        row_ids = block_index * block_rows + jnp.arange(block_rows, dtype=jnp.int32)
        tables.append((row_ids[:, None] == flat_place[None, :]).astype(jnp.bfloat16))
    return tables


def slots_to_order(tables, arrived_flat):
    return jnp.concatenate(
        [
            jnp.dot(table, arrived_flat, preferred_element_type=jnp.float32).astype(jnp.bfloat16)
            for table in tables
        ],
        axis=0,
    )


def order_to_slots(tables, result_flat, block_rows):
    total = None
    for block_index, table in enumerate(tables):
        piece = result_flat[block_index * block_rows : (block_index + 1) * block_rows]
        term = jnp.einsum("la,lf->af", table, piece, preferred_element_type=jnp.float32)
        total = term if total is None else total + term
    return total.astype(jnp.bfloat16)


def slots_to_rows(returned, local_slot):
    head_count = returned.shape[0]
    flat_rows = returned.reshape(head_count, -1, returned.shape[-1])
    slot_ids = jnp.arange(flat_rows.shape[1], dtype=jnp.int32)
    hits = (local_slot[:, :, None] == slot_ids[None, None, :]).astype(jnp.bfloat16)
    return jnp.einsum("rhs,hsf->rhf", hits, flat_rows, preferred_element_type=jnp.float32).astype(
        jnp.bfloat16
    )


def masked_scores(query_part, key_part, row_start, score_scale):
    scores = (
        jnp.einsum("qd,kd->qk", query_part, key_part, preferred_element_type=jnp.float32)
        * score_scale
    )
    row_ids = row_start + lax.broadcasted_iota(jnp.int32, scores.shape, 0)
    col_ids = lax.broadcasted_iota(jnp.int32, scores.shape, 1)
    return jnp.where(col_ids <= row_ids, scores, -jnp.inf)


def forward_pass(query_block, key_block, value_block, block_rows, score_scale):
    pieces, row_tops, row_totals = ([], [], [])
    for block_index in range(query_block.shape[0] // block_rows):
        row_start = block_index * block_rows
        finish = row_start + block_rows
        scores = masked_scores(
            query_block[row_start:finish], key_block[:finish], row_start, score_scale
        )
        row_top = jnp.max(scores, axis=1, keepdims=True)
        weights = jnp.exp(scores - row_top)
        row_total = jnp.sum(weights, axis=1, keepdims=True)
        probs_low = (weights / row_total).astype(jnp.bfloat16)
        pieces.append(
            jnp.dot(probs_low, value_block[:finish], preferred_element_type=jnp.float32).astype(
                jnp.bfloat16
            )
        )
        row_tops.append(row_top)
        row_totals.append(row_total)
    return (jnp.concatenate(pieces, axis=0), row_tops, row_totals)


def backward_pass(
    query_block,
    key_block,
    value_block,
    grad_block,
    attended_block,
    row_tops,
    row_totals,
    block_rows,
    score_scale,
):
    row_count, head_width = query_block.shape
    grad_key_sum = jnp.zeros((row_count, head_width), jnp.float32)
    grad_value_sum = jnp.zeros((row_count, head_width), jnp.float32)
    query_parts = []
    for block_index in range(row_count // block_rows):
        row_start = block_index * block_rows
        finish = row_start + block_rows
        scores = masked_scores(
            query_block[row_start:finish], key_block[:finish], row_start, score_scale
        )
        probabilities = jnp.exp(scores - row_tops[block_index]) / row_totals[block_index]
        probs_low = probabilities.astype(jnp.bfloat16)
        grad_part = grad_block[row_start:finish]
        grad_prob = jnp.einsum(
            "qd,kd->qk", grad_part, value_block[:finish], preferred_element_type=jnp.float32
        )
        row_delta = jnp.sum(
            grad_part.astype(jnp.float32) * attended_block[row_start:finish].astype(jnp.float32),
            axis=1,
            keepdims=True,
        )
        grad_score = (probabilities * (grad_prob - row_delta)).astype(jnp.bfloat16)
        query_parts.append(
            (
                jnp.dot(grad_score, key_block[:finish], preferred_element_type=jnp.float32)
                * score_scale
            ).astype(jnp.bfloat16)
        )
        key_term = jnp.einsum(
            "qk,qd->kd",
            grad_score,
            query_block[row_start:finish],
            preferred_element_type=jnp.float32,
        )
        value_term = jnp.einsum(
            "qk,qd->kd", probs_low, grad_part, preferred_element_type=jnp.float32
        )
        grad_key_sum = grad_key_sum + jnp.pad(key_term, ((0, row_count - finish), (0, 0)))
        grad_value_sum = grad_value_sum + jnp.pad(value_term, ((0, row_count - finish), (0, 0)))
    grad_query_block = jnp.concatenate(query_parts, axis=0)
    grad_key_block = (grad_key_sum * score_scale).astype(jnp.bfloat16)
    grad_value_block = grad_value_sum.astype(jnp.bfloat16)
    return jnp.stack((grad_query_block, grad_key_block, grad_value_block), axis=1)


def shards(query_rows, key_rows, value_rows, grad_rows, assignment, position):
    sub_rows, head_count, head_width = query_rows.shape
    clusters = lax.axis_size("seq")
    cluster_len = sub_rows * lax.axis_size("head")
    capacity = 3 * sub_rows // (2 * clusters)
    slot_count = clusters * capacity
    devices = clusters * head_count
    stacked = jnp.stack((query_rows, key_rows, value_rows, grad_rows), axis=2)
    local_slot = cluster_slots(assignment, clusters, capacity)
    group_rows = jnp.transpose(stacked.reshape(sub_rows, head_count, 4 * head_width), (1, 0, 2))
    packed, places = pack_slots(group_rows, local_slot.T, position.T, slot_count, cluster_len)
    packed = jnp.transpose(
        packed.reshape(head_count, clusters, capacity, 4 * head_width), (1, 0, 2, 3)
    ).reshape(devices, capacity * 4, head_width)
    places = jnp.transpose(places.reshape(head_count, clusters, capacity), (1, 0, 2)).reshape(
        devices, capacity
    )
    coded = jnp.concatenate((places // 32, places % 32), axis=1).astype(jnp.bfloat16)
    coded = jnp.pad(coded, ((0, 0), (0, 2 * head_width - 2 * capacity))).reshape(
        devices, 2, head_width
    )
    payload = jnp.concatenate((packed, coded), axis=1)
    rows = payload.shape[1]
    payload = payload.reshape(devices, rows // 2, 2, head_width)
    arrived = lax.all_to_all(payload, ("seq", "head"), 0, 0, tiled=True).reshape(
        devices, rows, head_width
    )
    arrived_data = arrived[:, : capacity * 4].reshape(devices * capacity, 4 * head_width)
    arrived_code = arrived[:, capacity * 4].astype(jnp.float32)
    flat_place = (
        arrived_code[:, :capacity] * 32.0 + arrived_code[:, capacity : 2 * capacity]
    ).astype(jnp.int32).reshape(-1)
    block_rows = min(512, cluster_len)
    tables = place_tables(flat_place, cluster_len, block_rows)
    ordered = slots_to_order(tables, arrived_data).reshape(cluster_len, 4, head_width)
    query_block = ordered[:, 0]
    key_block = ordered[:, 1]
    value_block = ordered[:, 2]
    grad_block = ordered[:, 3]
    score_scale = 1.0 / math.sqrt(head_width)
    attended_block, row_tops, row_totals = forward_pass(
        query_block, key_block, value_block, block_rows, score_scale
    )
    grads_block = backward_pass(
        query_block,
        key_block,
        value_block,
        grad_block,
        attended_block,
        row_tops,
        row_totals,
        block_rows,
        score_scale,
    )
    combined = jnp.concatenate((attended_block[:, None], grads_block), axis=1).reshape(
        cluster_len, 4 * head_width
    )
    all_slots = order_to_slots(tables, combined, block_rows).reshape(
        devices, capacity, 4, head_width
    )
    returned = lax.all_to_all(all_slots, ("seq", "head"), 0, 0, tiled=True)
    returned = jnp.transpose(
        returned.reshape(clusters, head_count, capacity, 4 * head_width), (1, 0, 2, 3)
    ).reshape(head_count, slot_count, 4 * head_width)
    everything = slots_to_rows(returned, local_slot).reshape(sub_rows, head_count, 4, head_width)
    return (everything[:, :, 0], everything[:, :, 1], everything[:, :, 2], everything[:, :, 3])


def solution(mesh):
    return jax.shard_map(
        shards,
        mesh=mesh,
        in_specs=(
            P(("seq", "head"), None, None),
            P(("seq", "head"), None, None),
            P(("seq", "head"), None, None),
            P(("seq", "head"), None, None),
            P(("seq", "head"), None),
            P(("seq", "head"), None),
        ),
        out_specs=(
            P(("seq", "head"), None, None),
            P(("seq", "head"), None, None),
            P(("seq", "head"), None, None),
            P(("seq", "head"), None, None),
        ),
        check_vma=False,
    )
```

```python
import math

import jax
import jax.numpy as jnp
from jax import lax
from jax.sharding import PartitionSpec as P


def split_up(x, dim, devices):
    dims = x.shape
    parts = x.reshape(*dims[:dim], devices, dims[dim] // devices, *dims[dim + 1 :])
    return jnp.moveaxis(parts, dim, 0)


def in_order(parts, dim):
    dims = list(parts.shape[1:])
    dims[dim] *= parts.shape[0]
    return jnp.moveaxis(parts, 0, dim).reshape(dims)


def joined_exchange(x, axis, axes, splits, concats):
    sizes = [lax.axis_size(a) for a in axes]
    parts = split_up(x, splits[0], sizes[0])
    parts = jnp.moveaxis(split_up(parts, splits[1] + 1, sizes[1]), 0, 1)
    inside = parts.shape[2:]
    parts = parts.reshape(-1, *inside)
    parts = lax.all_to_all(parts, axis, split_axis=0, concat_axis=0, tiled=True)
    parts = in_order(parts.reshape(*sizes, *inside), concats[0] + 1)
    return in_order(parts, concats[1])


def cluster_slots(assign_cols, clusters, capacity):
    row_count, group_count = assign_cols.shape
    hits = assign_cols[:, :, None] == jnp.arange(clusters, dtype=jnp.int32)[None, None, :]
    onehot = hits.astype(jnp.bfloat16).reshape(row_count, group_count * clusters)
    lower = (
        lax.broadcasted_iota(jnp.int32, (row_count, row_count), 1)
        < lax.broadcasted_iota(jnp.int32, (row_count, row_count), 0)
    ).astype(jnp.bfloat16)
    earlier = jnp.dot(lower, onehot, preferred_element_type=jnp.float32).reshape(
        row_count, group_count, clusters
    )
    within = jnp.sum(jnp.where(hits, earlier, 0.0), axis=2).astype(jnp.int32)
    return assign_cols * capacity + within


def pack_slots(group_rows, group_slot, group_place, slot_count, empty_place):
    slot_ids = jnp.arange(slot_count, dtype=jnp.int32)
    hits = slot_ids[None, :, None] == group_slot[:, None, :]
    packed = jnp.einsum(
        "gsr,grf->gsf", hits.astype(jnp.bfloat16), group_rows, preferred_element_type=jnp.float32
    ).astype(jnp.bfloat16)
    filled = jnp.any(hits, axis=2)
    places = jnp.where(
        filled, jnp.sum(jnp.where(hits, group_place[:, None, :], 0), axis=2), empty_place
    )
    return (packed, places)


def place_tables(flat_place, cluster_len, block_rows):
    tables = []
    for block_index in range(cluster_len // block_rows):
        row_ids = block_index * block_rows + jnp.arange(block_rows, dtype=jnp.int32)
        tables.append((row_ids[:, None] == flat_place[None, :]).astype(jnp.bfloat16))
    return tables


def slots_to_order(tables, arrived_flat):
    return jnp.concatenate(
        [
            jnp.dot(table, arrived_flat, preferred_element_type=jnp.float32).astype(jnp.bfloat16)
            for table in tables
        ],
        axis=0,
    )


def order_to_slots(tables, result_flat, block_rows):
    total = None
    for block_index, table in enumerate(tables):
        piece = result_flat[block_index * block_rows : (block_index + 1) * block_rows]
        term = jnp.einsum("la,lf->af", table, piece, preferred_element_type=jnp.float32)
        total = term if total is None else total + term
    return total.astype(jnp.bfloat16)


def slots_to_rows(returned, local_slot):
    head_count = returned.shape[0]
    flat_rows = returned.reshape(head_count, -1, returned.shape[-1])
    slot_ids = jnp.arange(flat_rows.shape[1], dtype=jnp.int32)
    hits = (local_slot[:, :, None] == slot_ids[None, None, :]).astype(jnp.bfloat16)
    return jnp.einsum("rhs,hsf->rhf", hits, flat_rows, preferred_element_type=jnp.float32).astype(
        jnp.bfloat16
    )


def masked_scores(query_part, key_part, row_start, score_scale):
    scores = (
        jnp.einsum("qd,kd->qk", query_part, key_part, preferred_element_type=jnp.float32)
        * score_scale
    )
    row_ids = row_start + lax.broadcasted_iota(jnp.int32, scores.shape, 0)
    col_ids = lax.broadcasted_iota(jnp.int32, scores.shape, 1)
    return jnp.where(col_ids <= row_ids, scores, -jnp.inf)


def forward_pass(query_block, key_block, value_block, block_rows, score_scale):
    pieces, row_tops, row_totals = ([], [], [])
    for block_index in range(query_block.shape[0] // block_rows):
        row_start = block_index * block_rows
        finish = row_start + block_rows
        scores = masked_scores(
            query_block[row_start:finish], key_block[:finish], row_start, score_scale
        )
        row_top = jnp.max(scores, axis=1, keepdims=True)
        weights = jnp.exp(scores - row_top)
        row_total = jnp.sum(weights, axis=1, keepdims=True)
        probs_low = (weights / row_total).astype(jnp.bfloat16)
        pieces.append(
            jnp.dot(probs_low, value_block[:finish], preferred_element_type=jnp.float32).astype(
                jnp.bfloat16
            )
        )
        row_tops.append(row_top)
        row_totals.append(row_total)
    return (jnp.concatenate(pieces, axis=0), row_tops, row_totals)


def backward_pass(
    query_block,
    key_block,
    value_block,
    grad_block,
    attended_block,
    row_tops,
    row_totals,
    block_rows,
    score_scale,
):
    row_count, head_width = query_block.shape
    grad_key_sum = jnp.zeros((row_count, head_width), jnp.float32)
    grad_value_sum = jnp.zeros((row_count, head_width), jnp.float32)
    query_parts = []
    for block_index in range(row_count // block_rows):
        row_start = block_index * block_rows
        finish = row_start + block_rows
        scores = masked_scores(
            query_block[row_start:finish], key_block[:finish], row_start, score_scale
        )
        probabilities = jnp.exp(scores - row_tops[block_index]) / row_totals[block_index]
        probs_low = probabilities.astype(jnp.bfloat16)
        grad_part = grad_block[row_start:finish]
        grad_prob = jnp.einsum(
            "qd,kd->qk", grad_part, value_block[:finish], preferred_element_type=jnp.float32
        )
        row_delta = jnp.sum(
            grad_part.astype(jnp.float32) * attended_block[row_start:finish].astype(jnp.float32),
            axis=1,
            keepdims=True,
        )
        grad_score = (probabilities * (grad_prob - row_delta)).astype(jnp.bfloat16)
        query_parts.append(
            (
                jnp.dot(grad_score, key_block[:finish], preferred_element_type=jnp.float32)
                * score_scale
            ).astype(jnp.bfloat16)
        )
        key_term = jnp.einsum(
            "qk,qd->kd",
            grad_score,
            query_block[row_start:finish],
            preferred_element_type=jnp.float32,
        )
        value_term = jnp.einsum(
            "qk,qd->kd", probs_low, grad_part, preferred_element_type=jnp.float32
        )
        grad_key_sum = grad_key_sum + jnp.pad(key_term, ((0, row_count - finish), (0, 0)))
        grad_value_sum = grad_value_sum + jnp.pad(value_term, ((0, row_count - finish), (0, 0)))
    grad_query_block = jnp.concatenate(query_parts, axis=0)
    grad_key_block = (grad_key_sum * score_scale).astype(jnp.bfloat16)
    grad_value_block = grad_value_sum.astype(jnp.bfloat16)
    return jnp.stack((grad_query_block, grad_key_block, grad_value_block), axis=1)


def shards(query_rows, key_rows, value_rows, grad_rows, assignment, position):
    sub_rows, head_count, head_width = query_rows.shape
    clusters = lax.axis_size("seq")
    cluster_len = sub_rows * lax.axis_size("head")
    capacity = 3 * sub_rows // (2 * clusters)
    slot_count = clusters * capacity
    devices = clusters * head_count
    order = ("head", "seq")
    local_slot = cluster_slots(assignment, clusters, capacity)
    slot_ids = jnp.arange(slot_count, dtype=jnp.int32)
    hits = slot_ids[None, :, None] == local_slot.T[:, None, :]
    hits_low = hits.astype(jnp.bfloat16)
    stacked = jnp.stack((query_rows, key_rows, value_rows, grad_rows), axis=2)
    packed = jnp.einsum(
        "hsr,rhaf->hsaf", hits_low, stacked, preferred_element_type=jnp.float32
    ).astype(jnp.bfloat16)
    places = jnp.where(
        jnp.any(hits, axis=2),
        jnp.sum(jnp.where(hits, position.T[:, None, :], 0), axis=2),
        cluster_len,
    ).reshape(devices, capacity)
    coded = jnp.concatenate((places // 32, places % 32), axis=1).astype(jnp.bfloat16)
    coded = jnp.pad(coded, ((0, 0), (0, 2 * head_width - 2 * capacity))).reshape(
        devices, 1, 2, head_width
    )
    payload = jnp.concatenate(
        (packed.reshape(devices, capacity * 2, 2, head_width), coded), axis=1
    )
    rows = 2 * payload.shape[1]
    arrived = lax.all_to_all(payload, order, 0, 0, tiled=True).reshape(devices, rows, head_width)
    arrived_data = arrived[:, : capacity * 4].reshape(devices * capacity, 4 * head_width)
    arrived_code = arrived[:, capacity * 4].astype(jnp.float32)
    flat_place = (
        arrived_code[:, :capacity] * 32.0 + arrived_code[:, capacity : 2 * capacity]
    ).astype(jnp.int32).reshape(-1)
    block_rows = min(512, cluster_len)
    tables = place_tables(flat_place, cluster_len, block_rows)
    ordered = slots_to_order(tables, arrived_data).reshape(cluster_len, 4, head_width)
    query_block = ordered[:, 0]
    key_block = ordered[:, 1]
    value_block = ordered[:, 2]
    grad_block = ordered[:, 3]
    score_scale = 1.0 / math.sqrt(head_width)
    attended_block, row_tops, row_totals = forward_pass(
        query_block, key_block, value_block, block_rows, score_scale
    )
    grads_block = backward_pass(
        query_block,
        key_block,
        value_block,
        grad_block,
        attended_block,
        row_tops,
        row_totals,
        block_rows,
        score_scale,
    )
    combined = jnp.concatenate((attended_block[:, None], grads_block), axis=1).reshape(
        cluster_len, 4 * head_width
    )
    all_slots = order_to_slots(tables, combined, block_rows).reshape(
        devices, capacity, 4, head_width
    )
    returned = lax.all_to_all(all_slots, order, 0, 0, tiled=True).reshape(
        head_count, slot_count, 4, head_width
    )
    return tuple(
        jnp.stack(
            [
                jnp.dot(
                    hits_low[head].T, returned[head, :, member], preferred_element_type=jnp.float32
                ).astype(jnp.bfloat16)
                for head in range(head_count)
            ],
            axis=1,
        )
        for member in range(4)
    )


def solution(mesh):
    return jax.shard_map(
        shards,
        mesh=mesh,
        in_specs=(
            P(("seq", "head"), None, None),
            P(("seq", "head"), None, None),
            P(("seq", "head"), None, None),
            P(("seq", "head"), None, None),
            P(("seq", "head"), None),
            P(("seq", "head"), None),
        ),
        out_specs=(
            P(("seq", "head"), None, None),
            P(("seq", "head"), None, None),
            P(("seq", "head"), None, None),
            P(("seq", "head"), None, None),
        ),
        check_vma=False,
    )
```

```python
import math

import jax
import jax.numpy as jnp
from jax import lax
from jax.sharding import PartitionSpec as P


def split_up(x, dim, devices):
    dims = x.shape
    parts = x.reshape(*dims[:dim], devices, dims[dim] // devices, *dims[dim + 1 :])
    return jnp.moveaxis(parts, dim, 0)


def in_order(parts, dim):
    dims = list(parts.shape[1:])
    dims[dim] *= parts.shape[0]
    return jnp.moveaxis(parts, 0, dim).reshape(dims)


def joined_exchange(x, axis, axes, splits, concats):
    sizes = [lax.axis_size(a) for a in axes]
    parts = split_up(x, splits[0], sizes[0])
    parts = jnp.moveaxis(split_up(parts, splits[1] + 1, sizes[1]), 0, 1)
    inside = parts.shape[2:]
    parts = parts.reshape(-1, *inside)
    parts = lax.all_to_all(parts, axis, split_axis=0, concat_axis=0, tiled=True)
    parts = in_order(parts.reshape(*sizes, *inside), concats[0] + 1)
    return in_order(parts, concats[1])


def cluster_slots(assign_cols, clusters, capacity):
    row_count, group_count = assign_cols.shape
    hits = assign_cols[:, :, None] == jnp.arange(clusters, dtype=jnp.int32)[None, None, :]
    onehot = hits.astype(jnp.bfloat16).reshape(row_count, group_count * clusters)
    lower = (
        lax.broadcasted_iota(jnp.int32, (row_count, row_count), 1)
        < lax.broadcasted_iota(jnp.int32, (row_count, row_count), 0)
    ).astype(jnp.bfloat16)
    earlier = jnp.dot(lower, onehot, preferred_element_type=jnp.float32).reshape(
        row_count, group_count, clusters
    )
    within = jnp.sum(jnp.where(hits, earlier, 0.0), axis=2).astype(jnp.int32)
    return assign_cols * capacity + within


def pack_slots(group_rows, group_slot, group_place, slot_count, empty_place):
    slot_ids = jnp.arange(slot_count, dtype=jnp.int32)
    hits = slot_ids[None, :, None] == group_slot[:, None, :]
    packed = jnp.einsum(
        "gsr,grf->gsf", hits.astype(jnp.bfloat16), group_rows, preferred_element_type=jnp.float32
    ).astype(jnp.bfloat16)
    filled = jnp.any(hits, axis=2)
    places = jnp.where(
        filled, jnp.sum(jnp.where(hits, group_place[:, None, :], 0), axis=2), empty_place
    )
    return (packed, places)


def place_tables(flat_place, cluster_len, block_rows):
    tables = []
    for block_index in range(cluster_len // block_rows):
        row_ids = block_index * block_rows + jnp.arange(block_rows, dtype=jnp.int32)
        tables.append((row_ids[:, None] == flat_place[None, :]).astype(jnp.bfloat16))
    return tables


def slots_to_order(tables, arrived_flat):
    return jnp.concatenate(
        [
            jnp.dot(table, arrived_flat, preferred_element_type=jnp.float32).astype(jnp.bfloat16)
            for table in tables
        ],
        axis=0,
    )


def order_to_slots(tables, result_flat, block_rows):
    total = None
    for block_index, table in enumerate(tables):
        piece = result_flat[block_index * block_rows : (block_index + 1) * block_rows]
        term = jnp.einsum("la,lf->af", table, piece, preferred_element_type=jnp.float32)
        total = term if total is None else total + term
    return total.astype(jnp.bfloat16)


def slots_to_rows(returned, local_slot):
    head_count = returned.shape[0]
    flat_rows = returned.reshape(head_count, -1, returned.shape[-1])
    slot_ids = jnp.arange(flat_rows.shape[1], dtype=jnp.int32)
    hits = (local_slot[:, :, None] == slot_ids[None, None, :]).astype(jnp.bfloat16)
    return jnp.einsum("rhs,hsf->rhf", hits, flat_rows, preferred_element_type=jnp.float32).astype(
        jnp.bfloat16
    )


def masked_scores(query_part, key_part, row_start, score_scale):
    scores = (
        jnp.einsum("qd,kd->qk", query_part, key_part, preferred_element_type=jnp.float32)
        * score_scale
    )
    row_ids = row_start + lax.broadcasted_iota(jnp.int32, scores.shape, 0)
    col_ids = lax.broadcasted_iota(jnp.int32, scores.shape, 1)
    return jnp.where(col_ids <= row_ids, scores, -jnp.inf)


def forward_pass(query_block, key_block, value_block, block_rows, score_scale):
    pieces, row_tops, row_totals = ([], [], [])
    for block_index in range(query_block.shape[0] // block_rows):
        row_start = block_index * block_rows
        finish = row_start + block_rows
        scores = masked_scores(
            query_block[row_start:finish], key_block[:finish], row_start, score_scale
        )
        row_top = jnp.max(scores, axis=1, keepdims=True)
        weights = jnp.exp(scores - row_top)
        row_total = jnp.sum(weights, axis=1, keepdims=True)
        probs_low = (weights / row_total).astype(jnp.bfloat16)
        pieces.append(
            jnp.dot(probs_low, value_block[:finish], preferred_element_type=jnp.float32).astype(
                jnp.bfloat16
            )
        )
        row_tops.append(row_top)
        row_totals.append(row_total)
    return (jnp.concatenate(pieces, axis=0), row_tops, row_totals)


def backward_pass(
    query_block,
    key_block,
    value_block,
    grad_block,
    attended_block,
    row_tops,
    row_totals,
    block_rows,
    score_scale,
):
    row_count, head_width = query_block.shape
    grad_key_sum = jnp.zeros((row_count, head_width), jnp.float32)
    grad_value_sum = jnp.zeros((row_count, head_width), jnp.float32)
    query_parts = []
    for block_index in range(row_count // block_rows):
        row_start = block_index * block_rows
        finish = row_start + block_rows
        scores = masked_scores(
            query_block[row_start:finish], key_block[:finish], row_start, score_scale
        )
        probabilities = jnp.exp(scores - row_tops[block_index]) / row_totals[block_index]
        probs_low = probabilities.astype(jnp.bfloat16)
        grad_part = grad_block[row_start:finish]
        grad_prob = jnp.einsum(
            "qd,kd->qk", grad_part, value_block[:finish], preferred_element_type=jnp.float32
        )
        row_delta = jnp.sum(
            grad_part.astype(jnp.float32) * attended_block[row_start:finish].astype(jnp.float32),
            axis=1,
            keepdims=True,
        )
        grad_score = (probabilities * (grad_prob - row_delta)).astype(jnp.bfloat16)
        query_parts.append(
            (
                jnp.dot(grad_score, key_block[:finish], preferred_element_type=jnp.float32)
                * score_scale
            ).astype(jnp.bfloat16)
        )
        key_term = jnp.einsum(
            "qk,qd->kd",
            grad_score,
            query_block[row_start:finish],
            preferred_element_type=jnp.float32,
        )
        value_term = jnp.einsum(
            "qk,qd->kd", probs_low, grad_part, preferred_element_type=jnp.float32
        )
        grad_key_sum = grad_key_sum + jnp.pad(key_term, ((0, row_count - finish), (0, 0)))
        grad_value_sum = grad_value_sum + jnp.pad(value_term, ((0, row_count - finish), (0, 0)))
    grad_query_block = jnp.concatenate(query_parts, axis=0)
    grad_key_block = (grad_key_sum * score_scale).astype(jnp.bfloat16)
    grad_value_block = grad_value_sum.astype(jnp.bfloat16)
    return jnp.stack((grad_query_block, grad_key_block, grad_value_block), axis=1)


def shards(query_rows, key_rows, value_rows, grad_rows, assignment, position):
    sub_rows, head_count, head_width = query_rows.shape
    clusters = lax.axis_size("seq")
    cluster_len = sub_rows * lax.axis_size("head")
    capacity = 3 * sub_rows // (2 * clusters)
    slot_count = clusters * capacity
    devices = clusters * head_count
    order = ("head", "seq")
    local_slot = cluster_slots(assignment, clusters, capacity)
    slot_ids = jnp.arange(slot_count, dtype=jnp.int32)
    hits = slot_ids[None, :, None] == local_slot.T[:, None, :]
    hits_low = hits.astype(jnp.bfloat16)
    stacked = jnp.stack((query_rows, key_rows, value_rows, grad_rows), axis=2)
    packed = jnp.einsum(
        "hsr,rhaf->hsaf", hits_low, stacked, preferred_element_type=jnp.float32
    ).astype(jnp.bfloat16)
    places = jnp.where(
        jnp.any(hits, axis=2),
        jnp.sum(jnp.where(hits, position.T[:, None, :], 0), axis=2),
        cluster_len,
    ).reshape(devices, capacity)
    coded = jnp.concatenate((places // 32, places % 32), axis=1).astype(jnp.bfloat16)
    coded = jnp.pad(coded, ((0, 0), (0, 2 * head_width - 2 * capacity))).reshape(
        devices, 1, 2, head_width
    )
    payload = jnp.concatenate(
        (packed.reshape(devices, capacity * 2, 2, head_width), coded), axis=1
    )
    rows = 2 * payload.shape[1]
    arrived = lax.all_to_all(payload, order, 0, 0, tiled=True).reshape(devices, rows, head_width)
    arrived_data = arrived[:, : capacity * 4].reshape(devices * capacity, 4 * head_width)
    arrived_code = arrived[:, capacity * 4].astype(jnp.float32)
    flat_place = (
        arrived_code[:, :capacity] * 32.0 + arrived_code[:, capacity : 2 * capacity]
    ).astype(jnp.int32).reshape(-1)
    block_rows = min(512, cluster_len)
    tables = place_tables(flat_place, cluster_len, block_rows)
    ordered = slots_to_order(tables, arrived_data).reshape(cluster_len, 4, head_width)
    query_block = ordered[:, 0]
    key_block = ordered[:, 1]
    value_block = ordered[:, 2]
    grad_block = ordered[:, 3]
    score_scale = 1.0 / math.sqrt(head_width)
    attended_block, row_tops, row_totals = forward_pass(
        query_block, key_block, value_block, block_rows, score_scale
    )
    grads_block = backward_pass(
        query_block,
        key_block,
        value_block,
        grad_block,
        attended_block,
        row_tops,
        row_totals,
        block_rows,
        score_scale,
    )
    combined = jnp.concatenate((attended_block[:, None], grads_block), axis=1).reshape(
        cluster_len, 4 * head_width
    )
    all_slots = order_to_slots(tables, combined, block_rows).reshape(
        devices, capacity, 4, head_width
    )
    returned = lax.all_to_all(all_slots, order, 0, 0, tiled=True).reshape(
        devices * capacity, 4, head_width
    )
    back_target = (jnp.arange(head_count, dtype=jnp.int32)[None, :] * slot_count + local_slot).reshape(-1)
    back_hits = (
        jnp.arange(devices * capacity, dtype=jnp.int32)[None, :] == back_target[:, None]
    ).astype(jnp.bfloat16)
    return tuple(
        jnp.dot(back_hits, returned[:, member], preferred_element_type=jnp.float32)
        .astype(jnp.bfloat16)
        .reshape(sub_rows, head_count, head_width)
        for member in range(4)
    )


def solution(mesh):
    return jax.shard_map(
        shards,
        mesh=mesh,
        in_specs=(
            P(("seq", "head"), None, None),
            P(("seq", "head"), None, None),
            P(("seq", "head"), None, None),
            P(("seq", "head"), None, None),
            P(("seq", "head"), None),
            P(("seq", "head"), None),
        ),
        out_specs=(
            P(("seq", "head"), None, None),
            P(("seq", "head"), None, None),
            P(("seq", "head"), None, None),
            P(("seq", "head"), None, None),
        ),
        check_vma=False,
    )
```

```python
import math

import jax
import jax.numpy as jnp
from jax import lax
from jax.sharding import PartitionSpec as P


def split_up(x, dim, devices):
    dims = x.shape
    parts = x.reshape(*dims[:dim], devices, dims[dim] // devices, *dims[dim + 1 :])
    return jnp.moveaxis(parts, dim, 0)


def in_order(parts, dim):
    dims = list(parts.shape[1:])
    dims[dim] *= parts.shape[0]
    return jnp.moveaxis(parts, 0, dim).reshape(dims)


def joined_exchange(x, axis, axes, splits, concats):
    sizes = [lax.axis_size(a) for a in axes]
    parts = split_up(x, splits[0], sizes[0])
    parts = jnp.moveaxis(split_up(parts, splits[1] + 1, sizes[1]), 0, 1)
    inside = parts.shape[2:]
    parts = parts.reshape(-1, *inside)
    parts = lax.all_to_all(parts, axis, split_axis=0, concat_axis=0, tiled=True)
    parts = in_order(parts.reshape(*sizes, *inside), concats[0] + 1)
    return in_order(parts, concats[1])


def cluster_slots(assign_cols, clusters, capacity):
    row_count, group_count = assign_cols.shape
    hits = assign_cols[:, :, None] == jnp.arange(clusters, dtype=jnp.int32)[None, None, :]
    onehot = hits.astype(jnp.bfloat16).reshape(row_count, group_count * clusters)
    lower = (
        lax.broadcasted_iota(jnp.int32, (row_count, row_count), 1)
        < lax.broadcasted_iota(jnp.int32, (row_count, row_count), 0)
    ).astype(jnp.bfloat16)
    earlier = jnp.dot(lower, onehot, preferred_element_type=jnp.float32).reshape(
        row_count, group_count, clusters
    )
    within = jnp.sum(jnp.where(hits, earlier, 0.0), axis=2).astype(jnp.int32)
    return assign_cols * capacity + within


def pack_slots(group_rows, group_slot, group_place, slot_count, empty_place):
    slot_ids = jnp.arange(slot_count, dtype=jnp.int32)
    hits = slot_ids[None, :, None] == group_slot[:, None, :]
    packed = jnp.einsum(
        "gsr,grf->gsf", hits.astype(jnp.bfloat16), group_rows, preferred_element_type=jnp.float32
    ).astype(jnp.bfloat16)
    filled = jnp.any(hits, axis=2)
    places = jnp.where(
        filled, jnp.sum(jnp.where(hits, group_place[:, None, :], 0), axis=2), empty_place
    )
    return (packed, places)


def place_tables(flat_place, cluster_len, block_rows):
    tables = []
    for block_index in range(cluster_len // block_rows):
        row_ids = block_index * block_rows + jnp.arange(block_rows, dtype=jnp.int32)
        tables.append((row_ids[:, None] == flat_place[None, :]).astype(jnp.bfloat16))
    return tables


def slots_to_order(tables, arrived_flat):
    return jnp.concatenate(
        [
            jnp.dot(table, arrived_flat, preferred_element_type=jnp.float32).astype(jnp.bfloat16)
            for table in tables
        ],
        axis=0,
    )


def order_to_slots(tables, result_flat, block_rows):
    total = None
    for block_index, table in enumerate(tables):
        piece = result_flat[block_index * block_rows : (block_index + 1) * block_rows]
        term = jnp.einsum("la,lf->af", table, piece, preferred_element_type=jnp.float32)
        total = term if total is None else total + term
    return total.astype(jnp.bfloat16)


def slots_to_rows(returned, local_slot):
    head_count = returned.shape[0]
    flat_rows = returned.reshape(head_count, -1, returned.shape[-1])
    slot_ids = jnp.arange(flat_rows.shape[1], dtype=jnp.int32)
    hits = (local_slot[:, :, None] == slot_ids[None, None, :]).astype(jnp.bfloat16)
    return jnp.einsum("rhs,hsf->rhf", hits, flat_rows, preferred_element_type=jnp.float32).astype(
        jnp.bfloat16
    )


def masked_scores(query_part, key_part, row_start, score_scale):
    scores = (
        jnp.einsum("qd,kd->qk", query_part, key_part, preferred_element_type=jnp.float32)
        * score_scale
    )
    row_ids = row_start + lax.broadcasted_iota(jnp.int32, scores.shape, 0)
    col_ids = lax.broadcasted_iota(jnp.int32, scores.shape, 1)
    return jnp.where(col_ids <= row_ids, scores, -jnp.inf)


def forward_pass(query_block, key_block, value_block, block_rows, score_scale):
    pieces, row_tops, row_totals = ([], [], [])
    for block_index in range(query_block.shape[0] // block_rows):
        row_start = block_index * block_rows
        finish = row_start + block_rows
        scores = masked_scores(
            query_block[row_start:finish], key_block[:finish], row_start, score_scale
        )
        row_top = jnp.max(scores, axis=1, keepdims=True)
        weights = jnp.exp(scores - row_top)
        row_total = jnp.sum(weights, axis=1, keepdims=True)
        probs_low = (weights / row_total).astype(jnp.bfloat16)
        pieces.append(
            jnp.dot(probs_low, value_block[:finish], preferred_element_type=jnp.float32).astype(
                jnp.bfloat16
            )
        )
        row_tops.append(row_top)
        row_totals.append(row_total)
    return (jnp.concatenate(pieces, axis=0), row_tops, row_totals)


def backward_pass(
    query_block,
    key_block,
    value_block,
    grad_block,
    attended_block,
    row_tops,
    row_totals,
    block_rows,
    score_scale,
):
    row_count, head_width = query_block.shape
    grad_key_sum = jnp.zeros((row_count, head_width), jnp.float32)
    grad_value_sum = jnp.zeros((row_count, head_width), jnp.float32)
    query_parts = []
    for block_index in range(row_count // block_rows):
        row_start = block_index * block_rows
        finish = row_start + block_rows
        scores = masked_scores(
            query_block[row_start:finish], key_block[:finish], row_start, score_scale
        )
        probabilities = jnp.exp(scores - row_tops[block_index]) / row_totals[block_index]
        probs_low = probabilities.astype(jnp.bfloat16)
        grad_part = grad_block[row_start:finish]
        grad_prob = jnp.einsum(
            "qd,kd->qk", grad_part, value_block[:finish], preferred_element_type=jnp.float32
        )
        row_delta = jnp.sum(
            grad_part.astype(jnp.float32) * attended_block[row_start:finish].astype(jnp.float32),
            axis=1,
            keepdims=True,
        )
        grad_score = (probabilities * (grad_prob - row_delta)).astype(jnp.bfloat16)
        query_parts.append(
            (
                jnp.dot(grad_score, key_block[:finish], preferred_element_type=jnp.float32)
                * score_scale
            ).astype(jnp.bfloat16)
        )
        key_term = jnp.einsum(
            "qk,qd->kd",
            grad_score,
            query_block[row_start:finish],
            preferred_element_type=jnp.float32,
        )
        value_term = jnp.einsum(
            "qk,qd->kd", probs_low, grad_part, preferred_element_type=jnp.float32
        )
        grad_key_sum = grad_key_sum + jnp.pad(key_term, ((0, row_count - finish), (0, 0)))
        grad_value_sum = grad_value_sum + jnp.pad(value_term, ((0, row_count - finish), (0, 0)))
    grad_query_block = jnp.concatenate(query_parts, axis=0)
    grad_key_block = (grad_key_sum * score_scale).astype(jnp.bfloat16)
    grad_value_block = grad_value_sum.astype(jnp.bfloat16)
    return jnp.stack((grad_query_block, grad_key_block, grad_value_block), axis=1)


def shards(query_rows, key_rows, value_rows, grad_rows, assignment, position):
    sub_rows, head_count, head_width = query_rows.shape
    clusters = lax.axis_size("seq")
    cluster_len = sub_rows * lax.axis_size("head")
    capacity = 3 * sub_rows // (2 * clusters)
    slot_count = clusters * capacity
    devices = clusters * head_count
    order = ("head", "seq")
    local_slot = cluster_slots(assignment, clusters, capacity)
    slot_ids = jnp.arange(slot_count, dtype=jnp.int32)
    hits = slot_ids[None, :, None] == local_slot.T[:, None, :]
    hits_low = hits.astype(jnp.bfloat16)
    stacked = jnp.stack((query_rows, key_rows, value_rows, grad_rows), axis=2)
    packed = jnp.einsum(
        "hsr,rhaf->hsaf", hits_low, stacked, preferred_element_type=jnp.float32
    ).astype(jnp.bfloat16)
    places = jnp.where(
        jnp.any(hits, axis=2),
        jnp.sum(jnp.where(hits, position.T[:, None, :], 0), axis=2),
        cluster_len,
    ).reshape(devices, capacity)
    coded = jnp.concatenate((places // 32, places % 32), axis=1).astype(jnp.bfloat16)
    coded = jnp.pad(coded, ((0, 0), (0, 2 * head_width - 2 * capacity))).reshape(
        devices, 1, 2, head_width
    )
    payload = jnp.concatenate(
        (packed.reshape(devices, capacity * 2, 2, head_width), coded), axis=1
    )
    rows = 2 * payload.shape[1]
    arrived = lax.all_to_all(payload, order, 0, 0, tiled=True).reshape(devices, rows, head_width)
    arrived_data = arrived[:, : capacity * 4].reshape(devices * capacity, 4 * head_width)
    arrived_code = arrived[:, capacity * 4].astype(jnp.float32)
    flat_place = (
        arrived_code[:, :capacity] * 32.0 + arrived_code[:, capacity : 2 * capacity]
    ).astype(jnp.int32).reshape(-1)
    block_rows = min(512, cluster_len)
    tables = place_tables(flat_place, cluster_len, block_rows)
    ordered = slots_to_order(tables, arrived_data).reshape(cluster_len, 4, head_width)
    query_block = ordered[:, 0]
    key_block = ordered[:, 1]
    value_block = ordered[:, 2]
    grad_block = ordered[:, 3]
    score_scale = 1.0 / math.sqrt(head_width)
    attended_block, row_tops, row_totals = forward_pass(
        query_block, key_block, value_block, block_rows, score_scale
    )
    grads_block = backward_pass(
        query_block,
        key_block,
        value_block,
        grad_block,
        attended_block,
        row_tops,
        row_totals,
        block_rows,
        score_scale,
    )
    combined = jnp.concatenate((attended_block[:, None], grads_block), axis=1).reshape(
        cluster_len, 4 * head_width
    )
    all_slots = order_to_slots(tables, combined, block_rows).reshape(
        devices, capacity, 4, head_width
    )
    returned = lax.all_to_all(all_slots, order, 0, 0, tiled=True).reshape(
        head_count, slot_count, 4 * head_width
    )
    everything = jnp.einsum(
        "hsr,hsf->rhf", hits_low, returned, preferred_element_type=jnp.float32
    ).astype(jnp.bfloat16).reshape(sub_rows, head_count, 4, head_width)
    return (everything[:, :, 0], everything[:, :, 1], everything[:, :, 2], everything[:, :, 3])


def solution(mesh):
    return jax.shard_map(
        shards,
        mesh=mesh,
        in_specs=(
            P(("seq", "head"), None, None),
            P(("seq", "head"), None, None),
            P(("seq", "head"), None, None),
            P(("seq", "head"), None, None),
            P(("seq", "head"), None),
            P(("seq", "head"), None),
        ),
        out_specs=(
            P(("seq", "head"), None, None),
            P(("seq", "head"), None, None),
            P(("seq", "head"), None, None),
            P(("seq", "head"), None, None),
        ),
        check_vma=False,
    )
```

```python
import functools
import math

import jax
import jax.numpy as jnp
from jax import lax
from jax.experimental import pallas as pl
from jax.experimental.pallas import tpu as pltpu
from jax.sharding import PartitionSpec as P


def split_up(x, dim, devices):
    dims = x.shape
    parts = x.reshape(*dims[:dim], devices, dims[dim] // devices, *dims[dim + 1 :])
    return jnp.moveaxis(parts, dim, 0)


def in_order(parts, dim):
    dims = list(parts.shape[1:])
    dims[dim] *= parts.shape[0]
    return jnp.moveaxis(parts, 0, dim).reshape(dims)


def joined_exchange(x, axis, axes, splits, concats):
    sizes = [lax.axis_size(a) for a in axes]
    parts = split_up(x, splits[0], sizes[0])
    parts = jnp.moveaxis(split_up(parts, splits[1] + 1, sizes[1]), 0, 1)
    inside = parts.shape[2:]
    parts = parts.reshape(-1, *inside)
    parts = lax.all_to_all(parts, axis, split_axis=0, concat_axis=0, tiled=True)
    parts = in_order(parts.reshape(*sizes, *inside), concats[0] + 1)
    return in_order(parts, concats[1])


def cluster_slots(assign_cols, clusters, capacity):
    row_count, group_count = assign_cols.shape
    hits = assign_cols[:, :, None] == jnp.arange(clusters, dtype=jnp.int32)[None, None, :]
    onehot = hits.astype(jnp.bfloat16).reshape(row_count, group_count * clusters)
    lower = (
        lax.broadcasted_iota(jnp.int32, (row_count, row_count), 1)
        < lax.broadcasted_iota(jnp.int32, (row_count, row_count), 0)
    ).astype(jnp.bfloat16)
    earlier = jnp.dot(lower, onehot, preferred_element_type=jnp.float32).reshape(
        row_count, group_count, clusters
    )
    within = jnp.sum(jnp.where(hits, earlier, 0.0), axis=2).astype(jnp.int32)
    return assign_cols * capacity + within


def pack_slots(group_rows, group_slot, group_place, slot_count, empty_place):
    slot_ids = jnp.arange(slot_count, dtype=jnp.int32)
    hits = slot_ids[None, :, None] == group_slot[:, None, :]
    packed = jnp.einsum(
        "gsr,grf->gsf", hits.astype(jnp.bfloat16), group_rows, preferred_element_type=jnp.float32
    ).astype(jnp.bfloat16)
    filled = jnp.any(hits, axis=2)
    places = jnp.where(
        filled, jnp.sum(jnp.where(hits, group_place[:, None, :], 0), axis=2), empty_place
    )
    return (packed, places)


def place_tables(flat_place, cluster_len, block_rows):
    tables = []
    for block_index in range(cluster_len // block_rows):
        row_ids = block_index * block_rows + jnp.arange(block_rows, dtype=jnp.int32)
        tables.append((row_ids[:, None] == flat_place[None, :]).astype(jnp.bfloat16))
    return tables


def slots_to_order(tables, arrived_flat):
    return jnp.concatenate(
        [
            jnp.dot(table, arrived_flat, preferred_element_type=jnp.float32).astype(jnp.bfloat16)
            for table in tables
        ],
        axis=0,
    )


def order_to_slots(tables, result_flat, block_rows):
    total = None
    for block_index, table in enumerate(tables):
        piece = result_flat[block_index * block_rows : (block_index + 1) * block_rows]
        term = jnp.einsum("la,lf->af", table, piece, preferred_element_type=jnp.float32)
        total = term if total is None else total + term
    return total.astype(jnp.bfloat16)


def slots_to_rows(returned, local_slot):
    head_count = returned.shape[0]
    flat_rows = returned.reshape(head_count, -1, returned.shape[-1])
    slot_ids = jnp.arange(flat_rows.shape[1], dtype=jnp.int32)
    hits = (local_slot[:, :, None] == slot_ids[None, None, :]).astype(jnp.bfloat16)
    return jnp.einsum("rhs,hsf->rhf", hits, flat_rows, preferred_element_type=jnp.float32).astype(
        jnp.bfloat16
    )


def masked_scores(query_part, key_part, row_start, score_scale):
    scores = (
        jnp.einsum("qd,kd->qk", query_part, key_part, preferred_element_type=jnp.float32)
        * score_scale
    )
    row_ids = row_start + lax.broadcasted_iota(jnp.int32, scores.shape, 0)
    col_ids = lax.broadcasted_iota(jnp.int32, scores.shape, 1)
    return jnp.where(col_ids <= row_ids, scores, -jnp.inf)


def forward_pass(query_block, key_block, value_block, block_rows, score_scale):
    pieces, row_tops, row_totals = ([], [], [])
    for block_index in range(query_block.shape[0] // block_rows):
        row_start = block_index * block_rows
        finish = row_start + block_rows
        scores = masked_scores(
            query_block[row_start:finish], key_block[:finish], row_start, score_scale
        )
        row_top = jnp.max(scores, axis=1, keepdims=True)
        weights = jnp.exp(scores - row_top)
        row_total = jnp.sum(weights, axis=1, keepdims=True)
        probs_low = (weights / row_total).astype(jnp.bfloat16)
        pieces.append(
            jnp.dot(probs_low, value_block[:finish], preferred_element_type=jnp.float32).astype(
                jnp.bfloat16
            )
        )
        row_tops.append(row_top)
        row_totals.append(row_total)
    return (jnp.concatenate(pieces, axis=0), row_tops, row_totals)


def backward_pass(
    query_block,
    key_block,
    value_block,
    grad_block,
    attended_block,
    row_tops,
    row_totals,
    block_rows,
    score_scale,
):
    row_count, head_width = query_block.shape
    grad_key_sum = jnp.zeros((row_count, head_width), jnp.float32)
    grad_value_sum = jnp.zeros((row_count, head_width), jnp.float32)
    query_parts = []
    for block_index in range(row_count // block_rows):
        row_start = block_index * block_rows
        finish = row_start + block_rows
        scores = masked_scores(
            query_block[row_start:finish], key_block[:finish], row_start, score_scale
        )
        probabilities = jnp.exp(scores - row_tops[block_index]) / row_totals[block_index]
        probs_low = probabilities.astype(jnp.bfloat16)
        grad_part = grad_block[row_start:finish]
        grad_prob = jnp.einsum(
            "qd,kd->qk", grad_part, value_block[:finish], preferred_element_type=jnp.float32
        )
        row_delta = jnp.sum(
            grad_part.astype(jnp.float32) * attended_block[row_start:finish].astype(jnp.float32),
            axis=1,
            keepdims=True,
        )
        grad_score = (probabilities * (grad_prob - row_delta)).astype(jnp.bfloat16)
        query_parts.append(
            (
                jnp.dot(grad_score, key_block[:finish], preferred_element_type=jnp.float32)
                * score_scale
            ).astype(jnp.bfloat16)
        )
        key_term = jnp.einsum(
            "qk,qd->kd",
            grad_score,
            query_block[row_start:finish],
            preferred_element_type=jnp.float32,
        )
        value_term = jnp.einsum(
            "qk,qd->kd", probs_low, grad_part, preferred_element_type=jnp.float32
        )
        grad_key_sum = grad_key_sum + jnp.pad(key_term, ((0, row_count - finish), (0, 0)))
        grad_value_sum = grad_value_sum + jnp.pad(value_term, ((0, row_count - finish), (0, 0)))
    grad_query_block = jnp.concatenate(query_parts, axis=0)
    grad_key_block = (grad_key_sum * score_scale).astype(jnp.bfloat16)
    grad_value_block = grad_value_sum.astype(jnp.bfloat16)
    return jnp.stack((grad_query_block, grad_key_block, grad_value_block), axis=1)


def attention_kernel(x_ref, out_ref, dk_acc, dv_acc, *, block_rows, head_width):
    rows = x_ref.shape[0]
    scale = 1.0 / math.sqrt(head_width)
    dk_acc[...] = jnp.zeros_like(dk_acc)
    dv_acc[...] = jnp.zeros_like(dv_acc)
    for block_index in range(rows // block_rows):
        start = block_index * block_rows
        finish = start + block_rows
        q_part = x_ref[start:finish, 0:head_width]
        g_part = x_ref[start:finish, 3 * head_width : 4 * head_width]
        k_seen = x_ref[0:finish, head_width : 2 * head_width]
        v_seen = x_ref[0:finish, 2 * head_width : 3 * head_width]
        scores = (
            lax.dot_general(q_part, k_seen, (((1,), (1,)), ((), ())), preferred_element_type=jnp.float32)
            * scale
        )
        row_ids = start + lax.broadcasted_iota(jnp.int32, scores.shape, 0)
        col_ids = lax.broadcasted_iota(jnp.int32, scores.shape, 1)
        scores = jnp.where(col_ids <= row_ids, scores, -jnp.inf)
        row_top = jnp.max(scores, axis=1, keepdims=True)
        weights = jnp.exp(scores - row_top)
        probabilities = weights / jnp.sum(weights, axis=1, keepdims=True)
        probs_low = probabilities.astype(jnp.bfloat16)
        attended = jnp.dot(probs_low, v_seen, preferred_element_type=jnp.float32).astype(jnp.bfloat16)
        out_ref[start:finish, 0:head_width] = attended
        grad_prob = lax.dot_general(
            g_part, v_seen, (((1,), (1,)), ((), ())), preferred_element_type=jnp.float32
        )
        row_delta = jnp.sum(
            g_part.astype(jnp.float32) * attended.astype(jnp.float32), axis=1, keepdims=True
        )
        grad_score = (probabilities * (grad_prob - row_delta)).astype(jnp.bfloat16)
        out_ref[start:finish, head_width : 2 * head_width] = (
            jnp.dot(grad_score, k_seen, preferred_element_type=jnp.float32) * scale
        ).astype(jnp.bfloat16)
        dk_acc[0:finish, :] += lax.dot_general(
            grad_score, q_part, (((0,), (0,)), ((), ())), preferred_element_type=jnp.float32
        )
        dv_acc[0:finish, :] += lax.dot_general(
            probs_low, g_part, (((0,), (0,)), ((), ())), preferred_element_type=jnp.float32
        )
    out_ref[:, 2 * head_width : 3 * head_width] = (dk_acc[...] * scale).astype(jnp.bfloat16)
    out_ref[:, 3 * head_width : 4 * head_width] = dv_acc[...].astype(jnp.bfloat16)


def fused_attention(ordered_flat, head_width, block_rows=256):
    rows, width = ordered_flat.shape
    return pl.pallas_call(
        functools.partial(attention_kernel, block_rows=block_rows, head_width=head_width),
        out_shape=jax.ShapeDtypeStruct((rows, width), jnp.bfloat16),
        scratch_shapes=[pltpu.VMEM((rows, head_width), jnp.float32)] * 2,
    )(ordered_flat)


def shards(query_rows, key_rows, value_rows, grad_rows, assignment, position):
    sub_rows, head_count, head_width = query_rows.shape
    clusters = lax.axis_size("seq")
    cluster_len = sub_rows * lax.axis_size("head")
    capacity = 3 * sub_rows // (2 * clusters)
    slot_count = clusters * capacity
    devices = clusters * head_count
    order = ("head", "seq")
    local_slot = cluster_slots(assignment, clusters, capacity)
    slot_ids = jnp.arange(slot_count, dtype=jnp.int32)
    hits = slot_ids[None, :, None] == local_slot.T[:, None, :]
    hits_low = hits.astype(jnp.bfloat16)
    stacked = jnp.stack((query_rows, key_rows, value_rows, grad_rows), axis=2)
    packed = jnp.einsum(
        "hsr,rhaf->hsaf", hits_low, stacked, preferred_element_type=jnp.float32
    ).astype(jnp.bfloat16)
    places = jnp.where(
        jnp.any(hits, axis=2),
        jnp.sum(jnp.where(hits, position.T[:, None, :], 0), axis=2),
        cluster_len,
    ).reshape(devices, capacity)
    coded = jnp.concatenate((places // 32, places % 32), axis=1).astype(jnp.bfloat16)
    coded = jnp.pad(coded, ((0, 0), (0, 2 * head_width - 2 * capacity))).reshape(
        devices, 1, 2, head_width
    )
    payload = jnp.concatenate(
        (packed.reshape(devices, capacity * 2, 2, head_width), coded), axis=1
    )
    rows = 2 * payload.shape[1]
    arrived = lax.all_to_all(payload, order, 0, 0, tiled=True).reshape(devices, rows, head_width)
    arrived_data = arrived[:, : capacity * 4].reshape(devices * capacity, 4 * head_width)
    arrived_code = arrived[:, capacity * 4].astype(jnp.float32)
    flat_place = (
        arrived_code[:, :capacity] * 32.0 + arrived_code[:, capacity : 2 * capacity]
    ).astype(jnp.int32).reshape(-1)
    block_rows = min(512, cluster_len)
    tables = place_tables(flat_place, cluster_len, block_rows)
    combined = fused_attention(slots_to_order(tables, arrived_data), head_width)
    all_slots = order_to_slots(tables, combined, block_rows).reshape(
        devices, capacity, 4, head_width
    )
    returned = lax.all_to_all(all_slots, order, 0, 0, tiled=True).reshape(
        head_count, slot_count, 4 * head_width
    )
    everything = jnp.einsum(
        "hsr,hsf->rhf", hits_low, returned, preferred_element_type=jnp.float32
    ).astype(jnp.bfloat16).reshape(sub_rows, head_count, 4, head_width)
    return (everything[:, :, 0], everything[:, :, 1], everything[:, :, 2], everything[:, :, 3])


def solution(mesh):
    return jax.shard_map(
        shards,
        mesh=mesh,
        in_specs=(
            P(("seq", "head"), None, None),
            P(("seq", "head"), None, None),
            P(("seq", "head"), None, None),
            P(("seq", "head"), None, None),
            P(("seq", "head"), None),
            P(("seq", "head"), None),
        ),
        out_specs=(
            P(("seq", "head"), None, None),
            P(("seq", "head"), None, None),
            P(("seq", "head"), None, None),
            P(("seq", "head"), None, None),
        ),
        check_vma=False,
    )
```

```python
import functools
import math

import jax
import jax.numpy as jnp
from jax import lax
from jax.experimental import pallas as pl
from jax.experimental.pallas import tpu as pltpu
from jax.sharding import PartitionSpec as P


def split_up(x, dim, devices):
    dims = x.shape
    parts = x.reshape(*dims[:dim], devices, dims[dim] // devices, *dims[dim + 1 :])
    return jnp.moveaxis(parts, dim, 0)


def in_order(parts, dim):
    dims = list(parts.shape[1:])
    dims[dim] *= parts.shape[0]
    return jnp.moveaxis(parts, 0, dim).reshape(dims)


def joined_exchange(x, axis, axes, splits, concats):
    sizes = [lax.axis_size(a) for a in axes]
    parts = split_up(x, splits[0], sizes[0])
    parts = jnp.moveaxis(split_up(parts, splits[1] + 1, sizes[1]), 0, 1)
    inside = parts.shape[2:]
    parts = parts.reshape(-1, *inside)
    parts = lax.all_to_all(parts, axis, split_axis=0, concat_axis=0, tiled=True)
    parts = in_order(parts.reshape(*sizes, *inside), concats[0] + 1)
    return in_order(parts, concats[1])


def cluster_slots(assign_cols, clusters, capacity):
    row_count, group_count = assign_cols.shape
    hits = assign_cols[:, :, None] == jnp.arange(clusters, dtype=jnp.int32)[None, None, :]
    onehot = hits.astype(jnp.bfloat16).reshape(row_count, group_count * clusters)
    lower = (
        lax.broadcasted_iota(jnp.int32, (row_count, row_count), 1)
        < lax.broadcasted_iota(jnp.int32, (row_count, row_count), 0)
    ).astype(jnp.bfloat16)
    earlier = jnp.dot(lower, onehot, preferred_element_type=jnp.float32).reshape(
        row_count, group_count, clusters
    )
    within = jnp.sum(jnp.where(hits, earlier, 0.0), axis=2).astype(jnp.int32)
    return assign_cols * capacity + within


def pack_slots(group_rows, group_slot, group_place, slot_count, empty_place):
    slot_ids = jnp.arange(slot_count, dtype=jnp.int32)
    hits = slot_ids[None, :, None] == group_slot[:, None, :]
    packed = jnp.einsum(
        "gsr,grf->gsf", hits.astype(jnp.bfloat16), group_rows, preferred_element_type=jnp.float32
    ).astype(jnp.bfloat16)
    filled = jnp.any(hits, axis=2)
    places = jnp.where(
        filled, jnp.sum(jnp.where(hits, group_place[:, None, :], 0), axis=2), empty_place
    )
    return (packed, places)


def place_tables(flat_place, cluster_len, block_rows):
    tables = []
    for block_index in range(cluster_len // block_rows):
        row_ids = block_index * block_rows + jnp.arange(block_rows, dtype=jnp.int32)
        tables.append((row_ids[:, None] == flat_place[None, :]).astype(jnp.bfloat16))
    return tables


def slots_to_order(tables, arrived_flat):
    return jnp.concatenate(
        [
            jnp.dot(table, arrived_flat, preferred_element_type=jnp.float32).astype(jnp.bfloat16)
            for table in tables
        ],
        axis=0,
    )


def order_to_slots(tables, result_flat, block_rows):
    total = None
    for block_index, table in enumerate(tables):
        piece = result_flat[block_index * block_rows : (block_index + 1) * block_rows]
        term = jnp.einsum("la,lf->af", table, piece, preferred_element_type=jnp.float32)
        total = term if total is None else total + term
    return total.astype(jnp.bfloat16)


def slots_to_rows(returned, local_slot):
    head_count = returned.shape[0]
    flat_rows = returned.reshape(head_count, -1, returned.shape[-1])
    slot_ids = jnp.arange(flat_rows.shape[1], dtype=jnp.int32)
    hits = (local_slot[:, :, None] == slot_ids[None, None, :]).astype(jnp.bfloat16)
    return jnp.einsum("rhs,hsf->rhf", hits, flat_rows, preferred_element_type=jnp.float32).astype(
        jnp.bfloat16
    )


def masked_scores(query_part, key_part, row_start, score_scale):
    scores = (
        jnp.einsum("qd,kd->qk", query_part, key_part, preferred_element_type=jnp.float32)
        * score_scale
    )
    row_ids = row_start + lax.broadcasted_iota(jnp.int32, scores.shape, 0)
    col_ids = lax.broadcasted_iota(jnp.int32, scores.shape, 1)
    return jnp.where(col_ids <= row_ids, scores, -jnp.inf)


def forward_pass(query_block, key_block, value_block, block_rows, score_scale):
    pieces, row_tops, row_totals = ([], [], [])
    for block_index in range(query_block.shape[0] // block_rows):
        row_start = block_index * block_rows
        finish = row_start + block_rows
        scores = masked_scores(
            query_block[row_start:finish], key_block[:finish], row_start, score_scale
        )
        row_top = jnp.max(scores, axis=1, keepdims=True)
        weights = jnp.exp(scores - row_top)
        row_total = jnp.sum(weights, axis=1, keepdims=True)
        probs_low = (weights / row_total).astype(jnp.bfloat16)
        pieces.append(
            jnp.dot(probs_low, value_block[:finish], preferred_element_type=jnp.float32).astype(
                jnp.bfloat16
            )
        )
        row_tops.append(row_top)
        row_totals.append(row_total)
    return (jnp.concatenate(pieces, axis=0), row_tops, row_totals)


def backward_pass(
    query_block,
    key_block,
    value_block,
    grad_block,
    attended_block,
    row_tops,
    row_totals,
    block_rows,
    score_scale,
):
    row_count, head_width = query_block.shape
    grad_key_sum = jnp.zeros((row_count, head_width), jnp.float32)
    grad_value_sum = jnp.zeros((row_count, head_width), jnp.float32)
    query_parts = []
    for block_index in range(row_count // block_rows):
        row_start = block_index * block_rows
        finish = row_start + block_rows
        scores = masked_scores(
            query_block[row_start:finish], key_block[:finish], row_start, score_scale
        )
        probabilities = jnp.exp(scores - row_tops[block_index]) / row_totals[block_index]
        probs_low = probabilities.astype(jnp.bfloat16)
        grad_part = grad_block[row_start:finish]
        grad_prob = jnp.einsum(
            "qd,kd->qk", grad_part, value_block[:finish], preferred_element_type=jnp.float32
        )
        row_delta = jnp.sum(
            grad_part.astype(jnp.float32) * attended_block[row_start:finish].astype(jnp.float32),
            axis=1,
            keepdims=True,
        )
        grad_score = (probabilities * (grad_prob - row_delta)).astype(jnp.bfloat16)
        query_parts.append(
            (
                jnp.dot(grad_score, key_block[:finish], preferred_element_type=jnp.float32)
                * score_scale
            ).astype(jnp.bfloat16)
        )
        key_term = jnp.einsum(
            "qk,qd->kd",
            grad_score,
            query_block[row_start:finish],
            preferred_element_type=jnp.float32,
        )
        value_term = jnp.einsum(
            "qk,qd->kd", probs_low, grad_part, preferred_element_type=jnp.float32
        )
        grad_key_sum = grad_key_sum + jnp.pad(key_term, ((0, row_count - finish), (0, 0)))
        grad_value_sum = grad_value_sum + jnp.pad(value_term, ((0, row_count - finish), (0, 0)))
    grad_query_block = jnp.concatenate(query_parts, axis=0)
    grad_key_block = (grad_key_sum * score_scale).astype(jnp.bfloat16)
    grad_value_block = grad_value_sum.astype(jnp.bfloat16)
    return jnp.stack((grad_query_block, grad_key_block, grad_value_block), axis=1)


def attention_kernel(place_ref, arrived_ref, out_ref, x_ref, y_ref, dk_acc, dv_acc, *, block_rows):
    rows, width = x_ref.shape
    head_width = width // 4
    scale = 1.0 / math.sqrt(head_width)
    order = (
        lax.broadcasted_iota(jnp.int32, (rows, place_ref.shape[1]), 0) == place_ref[...]
    ).astype(jnp.bfloat16)
    x_ref[...] = jnp.dot(order, arrived_ref[...], preferred_element_type=jnp.float32).astype(
        jnp.bfloat16
    )
    dk_acc[...] = jnp.zeros_like(dk_acc)
    dv_acc[...] = jnp.zeros_like(dv_acc)
    for block_index in range(rows // block_rows):
        start = block_index * block_rows
        finish = start + block_rows
        q_part = x_ref[start:finish, 0:head_width]
        g_part = x_ref[start:finish, 3 * head_width : 4 * head_width]
        k_seen = x_ref[0:finish, head_width : 2 * head_width]
        v_seen = x_ref[0:finish, 2 * head_width : 3 * head_width]
        scores = (
            lax.dot_general(q_part, k_seen, (((1,), (1,)), ((), ())), preferred_element_type=jnp.float32)
            * scale
        )
        row_ids = start + lax.broadcasted_iota(jnp.int32, scores.shape, 0)
        col_ids = lax.broadcasted_iota(jnp.int32, scores.shape, 1)
        scores = jnp.where(col_ids <= row_ids, scores, -jnp.inf)
        row_top = jnp.max(scores, axis=1, keepdims=True)
        weights = jnp.exp(scores - row_top)
        probabilities = weights / jnp.sum(weights, axis=1, keepdims=True)
        probs_low = probabilities.astype(jnp.bfloat16)
        attended = jnp.dot(probs_low, v_seen, preferred_element_type=jnp.float32).astype(jnp.bfloat16)
        y_ref[start:finish, 0:head_width] = attended
        grad_prob = lax.dot_general(
            g_part, v_seen, (((1,), (1,)), ((), ())), preferred_element_type=jnp.float32
        )
        row_delta = jnp.sum(
            g_part.astype(jnp.float32) * attended.astype(jnp.float32), axis=1, keepdims=True
        )
        grad_score = (probabilities * (grad_prob - row_delta)).astype(jnp.bfloat16)
        y_ref[start:finish, head_width : 2 * head_width] = (
            jnp.dot(grad_score, k_seen, preferred_element_type=jnp.float32) * scale
        ).astype(jnp.bfloat16)
        dk_acc[0:finish, :] += lax.dot_general(
            grad_score, q_part, (((0,), (0,)), ((), ())), preferred_element_type=jnp.float32
        )
        dv_acc[0:finish, :] += lax.dot_general(
            probs_low, g_part, (((0,), (0,)), ((), ())), preferred_element_type=jnp.float32
        )
    y_ref[:, 2 * head_width : 3 * head_width] = (dk_acc[...] * scale).astype(jnp.bfloat16)
    y_ref[:, 3 * head_width : 4 * head_width] = dv_acc[...].astype(jnp.bfloat16)
    out_ref[...] = lax.dot_general(
        order, y_ref[...], (((0,), (0,)), ((), ())), preferred_element_type=jnp.float32
    ).astype(jnp.bfloat16)


def fused_attention(flat_place, arrived_flat, cluster_len, block_rows=256):
    slots, width = arrived_flat.shape
    return pl.pallas_call(
        functools.partial(attention_kernel, block_rows=block_rows),
        out_shape=jax.ShapeDtypeStruct((slots, width), jnp.bfloat16),
        scratch_shapes=[
            pltpu.VMEM((cluster_len, width), jnp.bfloat16),
            pltpu.VMEM((cluster_len, width), jnp.bfloat16),
            pltpu.VMEM((cluster_len, width // 4), jnp.float32),
            pltpu.VMEM((cluster_len, width // 4), jnp.float32),
        ],
    )(flat_place.reshape(1, slots), arrived_flat)


def shards(query_rows, key_rows, value_rows, grad_rows, assignment, position):
    sub_rows, head_count, head_width = query_rows.shape
    clusters = lax.axis_size("seq")
    cluster_len = sub_rows * lax.axis_size("head")
    capacity = 3 * sub_rows // (2 * clusters)
    slot_count = clusters * capacity
    devices = clusters * head_count
    order = ("head", "seq")
    local_slot = cluster_slots(assignment, clusters, capacity)
    slot_ids = jnp.arange(slot_count, dtype=jnp.int32)
    hits = slot_ids[None, :, None] == local_slot.T[:, None, :]
    hits_low = hits.astype(jnp.bfloat16)
    stacked = jnp.stack((query_rows, key_rows, value_rows, grad_rows), axis=2)
    packed = jnp.einsum(
        "hsr,rhaf->hsaf", hits_low, stacked, preferred_element_type=jnp.float32
    ).astype(jnp.bfloat16)
    places = jnp.where(
        jnp.any(hits, axis=2),
        jnp.sum(jnp.where(hits, position.T[:, None, :], 0), axis=2),
        cluster_len,
    ).reshape(devices, capacity)
    coded = jnp.concatenate((places // 32, places % 32), axis=1).astype(jnp.bfloat16)
    coded = jnp.pad(coded, ((0, 0), (0, 2 * head_width - 2 * capacity))).reshape(
        devices, 1, 2, head_width
    )
    payload = jnp.concatenate(
        (packed.reshape(devices, capacity * 2, 2, head_width), coded), axis=1
    )
    rows = 2 * payload.shape[1]
    arrived = lax.all_to_all(payload, order, 0, 0, tiled=True).reshape(devices, rows, head_width)
    arrived_data = arrived[:, : capacity * 4].reshape(devices * capacity, 4 * head_width)
    arrived_code = arrived[:, capacity * 4].astype(jnp.float32)
    flat_place = (
        arrived_code[:, :capacity] * 32.0 + arrived_code[:, capacity : 2 * capacity]
    ).astype(jnp.int32).reshape(-1)
    all_slots = fused_attention(flat_place, arrived_data, cluster_len).reshape(
        devices, capacity, 4, head_width
    )
    returned = lax.all_to_all(all_slots, order, 0, 0, tiled=True).reshape(
        head_count, slot_count, 4 * head_width
    )
    everything = jnp.einsum(
        "hsr,hsf->rhf", hits_low, returned, preferred_element_type=jnp.float32
    ).astype(jnp.bfloat16).reshape(sub_rows, head_count, 4, head_width)
    return (everything[:, :, 0], everything[:, :, 1], everything[:, :, 2], everything[:, :, 3])


def solution(mesh):
    return jax.shard_map(
        shards,
        mesh=mesh,
        in_specs=(
            P(("seq", "head"), None, None),
            P(("seq", "head"), None, None),
            P(("seq", "head"), None, None),
            P(("seq", "head"), None, None),
            P(("seq", "head"), None),
            P(("seq", "head"), None),
        ),
        out_specs=(
            P(("seq", "head"), None, None),
            P(("seq", "head"), None, None),
            P(("seq", "head"), None, None),
            P(("seq", "head"), None, None),
        ),
        check_vma=False,
    )
```

```python
import functools
import math

import jax
import jax.numpy as jnp
from jax import lax
from jax.experimental import pallas as pl
from jax.experimental.pallas import tpu as pltpu
from jax.sharding import PartitionSpec as P


def split_up(x, dim, devices):
    dims = x.shape
    parts = x.reshape(*dims[:dim], devices, dims[dim] // devices, *dims[dim + 1 :])
    return jnp.moveaxis(parts, dim, 0)


def in_order(parts, dim):
    dims = list(parts.shape[1:])
    dims[dim] *= parts.shape[0]
    return jnp.moveaxis(parts, 0, dim).reshape(dims)


def joined_exchange(x, axis, axes, splits, concats):
    sizes = [lax.axis_size(a) for a in axes]
    parts = split_up(x, splits[0], sizes[0])
    parts = jnp.moveaxis(split_up(parts, splits[1] + 1, sizes[1]), 0, 1)
    inside = parts.shape[2:]
    parts = parts.reshape(-1, *inside)
    parts = lax.all_to_all(parts, axis, split_axis=0, concat_axis=0, tiled=True)
    parts = in_order(parts.reshape(*sizes, *inside), concats[0] + 1)
    return in_order(parts, concats[1])


def cluster_slots(assign_cols, clusters, capacity):
    row_count, group_count = assign_cols.shape
    hits = assign_cols[:, :, None] == jnp.arange(clusters, dtype=jnp.int32)[None, None, :]
    onehot = hits.astype(jnp.bfloat16).reshape(row_count, group_count * clusters)
    lower = (
        lax.broadcasted_iota(jnp.int32, (row_count, row_count), 1)
        < lax.broadcasted_iota(jnp.int32, (row_count, row_count), 0)
    ).astype(jnp.bfloat16)
    earlier = jnp.dot(lower, onehot, preferred_element_type=jnp.float32).reshape(
        row_count, group_count, clusters
    )
    within = jnp.sum(jnp.where(hits, earlier, 0.0), axis=2).astype(jnp.int32)
    return assign_cols * capacity + within


def pack_slots(group_rows, group_slot, group_place, slot_count, empty_place):
    slot_ids = jnp.arange(slot_count, dtype=jnp.int32)
    hits = slot_ids[None, :, None] == group_slot[:, None, :]
    packed = jnp.einsum(
        "gsr,grf->gsf", hits.astype(jnp.bfloat16), group_rows, preferred_element_type=jnp.float32
    ).astype(jnp.bfloat16)
    filled = jnp.any(hits, axis=2)
    places = jnp.where(
        filled, jnp.sum(jnp.where(hits, group_place[:, None, :], 0), axis=2), empty_place
    )
    return (packed, places)


def place_tables(flat_place, cluster_len, block_rows):
    tables = []
    for block_index in range(cluster_len // block_rows):
        row_ids = block_index * block_rows + jnp.arange(block_rows, dtype=jnp.int32)
        tables.append((row_ids[:, None] == flat_place[None, :]).astype(jnp.bfloat16))
    return tables


def slots_to_order(tables, arrived_flat):
    return jnp.concatenate(
        [
            jnp.dot(table, arrived_flat, preferred_element_type=jnp.float32).astype(jnp.bfloat16)
            for table in tables
        ],
        axis=0,
    )


def order_to_slots(tables, result_flat, block_rows):
    total = None
    for block_index, table in enumerate(tables):
        piece = result_flat[block_index * block_rows : (block_index + 1) * block_rows]
        term = jnp.einsum("la,lf->af", table, piece, preferred_element_type=jnp.float32)
        total = term if total is None else total + term
    return total.astype(jnp.bfloat16)


def slots_to_rows(returned, local_slot):
    head_count = returned.shape[0]
    flat_rows = returned.reshape(head_count, -1, returned.shape[-1])
    slot_ids = jnp.arange(flat_rows.shape[1], dtype=jnp.int32)
    hits = (local_slot[:, :, None] == slot_ids[None, None, :]).astype(jnp.bfloat16)
    return jnp.einsum("rhs,hsf->rhf", hits, flat_rows, preferred_element_type=jnp.float32).astype(
        jnp.bfloat16
    )


def masked_scores(query_part, key_part, row_start, score_scale):
    scores = (
        jnp.einsum("qd,kd->qk", query_part, key_part, preferred_element_type=jnp.float32)
        * score_scale
    )
    row_ids = row_start + lax.broadcasted_iota(jnp.int32, scores.shape, 0)
    col_ids = lax.broadcasted_iota(jnp.int32, scores.shape, 1)
    return jnp.where(col_ids <= row_ids, scores, -jnp.inf)


def forward_pass(query_block, key_block, value_block, block_rows, score_scale):
    pieces, row_tops, row_totals = ([], [], [])
    for block_index in range(query_block.shape[0] // block_rows):
        row_start = block_index * block_rows
        finish = row_start + block_rows
        scores = masked_scores(
            query_block[row_start:finish], key_block[:finish], row_start, score_scale
        )
        row_top = jnp.max(scores, axis=1, keepdims=True)
        weights = jnp.exp(scores - row_top)
        row_total = jnp.sum(weights, axis=1, keepdims=True)
        probs_low = (weights / row_total).astype(jnp.bfloat16)
        pieces.append(
            jnp.dot(probs_low, value_block[:finish], preferred_element_type=jnp.float32).astype(
                jnp.bfloat16
            )
        )
        row_tops.append(row_top)
        row_totals.append(row_total)
    return (jnp.concatenate(pieces, axis=0), row_tops, row_totals)


def backward_pass(
    query_block,
    key_block,
    value_block,
    grad_block,
    attended_block,
    row_tops,
    row_totals,
    block_rows,
    score_scale,
):
    row_count, head_width = query_block.shape
    grad_key_sum = jnp.zeros((row_count, head_width), jnp.float32)
    grad_value_sum = jnp.zeros((row_count, head_width), jnp.float32)
    query_parts = []
    for block_index in range(row_count // block_rows):
        row_start = block_index * block_rows
        finish = row_start + block_rows
        scores = masked_scores(
            query_block[row_start:finish], key_block[:finish], row_start, score_scale
        )
        probabilities = jnp.exp(scores - row_tops[block_index]) / row_totals[block_index]
        probs_low = probabilities.astype(jnp.bfloat16)
        grad_part = grad_block[row_start:finish]
        grad_prob = jnp.einsum(
            "qd,kd->qk", grad_part, value_block[:finish], preferred_element_type=jnp.float32
        )
        row_delta = jnp.sum(
            grad_part.astype(jnp.float32) * attended_block[row_start:finish].astype(jnp.float32),
            axis=1,
            keepdims=True,
        )
        grad_score = (probabilities * (grad_prob - row_delta)).astype(jnp.bfloat16)
        query_parts.append(
            (
                jnp.dot(grad_score, key_block[:finish], preferred_element_type=jnp.float32)
                * score_scale
            ).astype(jnp.bfloat16)
        )
        key_term = jnp.einsum(
            "qk,qd->kd",
            grad_score,
            query_block[row_start:finish],
            preferred_element_type=jnp.float32,
        )
        value_term = jnp.einsum(
            "qk,qd->kd", probs_low, grad_part, preferred_element_type=jnp.float32
        )
        grad_key_sum = grad_key_sum + jnp.pad(key_term, ((0, row_count - finish), (0, 0)))
        grad_value_sum = grad_value_sum + jnp.pad(value_term, ((0, row_count - finish), (0, 0)))
    grad_query_block = jnp.concatenate(query_parts, axis=0)
    grad_key_block = (grad_key_sum * score_scale).astype(jnp.bfloat16)
    grad_value_block = grad_value_sum.astype(jnp.bfloat16)
    return jnp.stack((grad_query_block, grad_key_block, grad_value_block), axis=1)


def attention_kernel(place_ref, place_col_ref, arrived_ref, out_ref, x_ref, y_ref, dk_acc, dv_acc, *, block_rows):
    rows, width = x_ref.shape
    head_width = width // 4
    scale = 1.0 / math.sqrt(head_width)
    order = (
        lax.broadcasted_iota(jnp.int32, (rows, place_ref.shape[1]), 0) == place_ref[...]
    ).astype(jnp.bfloat16)
    x_ref[...] = jnp.dot(order, arrived_ref[...], preferred_element_type=jnp.float32).astype(
        jnp.bfloat16
    )
    dk_acc[...] = jnp.zeros_like(dk_acc)
    dv_acc[...] = jnp.zeros_like(dv_acc)
    for block_index in range(rows // block_rows):
        start = block_index * block_rows
        finish = start + block_rows
        q_part = x_ref[start:finish, 0:head_width]
        g_part = x_ref[start:finish, 3 * head_width : 4 * head_width]
        k_seen = x_ref[0:finish, head_width : 2 * head_width]
        v_seen = x_ref[0:finish, 2 * head_width : 3 * head_width]
        scores = (
            lax.dot_general(q_part, k_seen, (((1,), (1,)), ((), ())), preferred_element_type=jnp.float32)
            * scale
        )
        row_ids = start + lax.broadcasted_iota(jnp.int32, scores.shape, 0)
        col_ids = lax.broadcasted_iota(jnp.int32, scores.shape, 1)
        scores = jnp.where(col_ids <= row_ids, scores, -jnp.inf)
        row_top = jnp.max(scores, axis=1, keepdims=True)
        weights = jnp.exp(scores - row_top)
        probabilities = weights / jnp.sum(weights, axis=1, keepdims=True)
        probs_low = probabilities.astype(jnp.bfloat16)
        attended = jnp.dot(probs_low, v_seen, preferred_element_type=jnp.float32).astype(jnp.bfloat16)
        y_ref[start:finish, 0:head_width] = attended
        grad_prob = lax.dot_general(
            g_part, v_seen, (((1,), (1,)), ((), ())), preferred_element_type=jnp.float32
        )
        row_delta = jnp.sum(
            g_part.astype(jnp.float32) * attended.astype(jnp.float32), axis=1, keepdims=True
        )
        grad_score = (probabilities * (grad_prob - row_delta)).astype(jnp.bfloat16)
        y_ref[start:finish, head_width : 2 * head_width] = (
            jnp.dot(grad_score, k_seen, preferred_element_type=jnp.float32) * scale
        ).astype(jnp.bfloat16)
        dk_acc[0:finish, :] += lax.dot_general(
            grad_score, q_part, (((0,), (0,)), ((), ())), preferred_element_type=jnp.float32
        )
        dv_acc[0:finish, :] += lax.dot_general(
            probs_low, g_part, (((0,), (0,)), ((), ())), preferred_element_type=jnp.float32
        )
    y_ref[:, 2 * head_width : 3 * head_width] = (dk_acc[...] * scale).astype(jnp.bfloat16)
    y_ref[:, 3 * head_width : 4 * head_width] = dv_acc[...].astype(jnp.bfloat16)
    back = (
        lax.broadcasted_iota(jnp.int32, (place_col_ref.shape[0], rows), 1) == place_col_ref[...]
    ).astype(jnp.bfloat16)
    out_ref[...] = jnp.dot(back, y_ref[...], preferred_element_type=jnp.float32).astype(
        jnp.bfloat16
    )


def fused_attention(flat_place, arrived_flat, cluster_len, block_rows=128):
    slots, width = arrived_flat.shape
    return pl.pallas_call(
        functools.partial(attention_kernel, block_rows=block_rows),
        out_shape=jax.ShapeDtypeStruct((slots, width), jnp.bfloat16),
        scratch_shapes=[
            pltpu.VMEM((cluster_len, width), jnp.bfloat16),
            pltpu.VMEM((cluster_len, width), jnp.bfloat16),
            pltpu.VMEM((cluster_len, width // 4), jnp.float32),
            pltpu.VMEM((cluster_len, width // 4), jnp.float32),
        ],
    )(flat_place.reshape(1, slots), flat_place.reshape(slots, 1), arrived_flat)


def shards(query_rows, key_rows, value_rows, grad_rows, assignment, position):
    sub_rows, head_count, head_width = query_rows.shape
    clusters = lax.axis_size("seq")
    cluster_len = sub_rows * lax.axis_size("head")
    capacity = 3 * sub_rows // (2 * clusters)
    slot_count = clusters * capacity
    devices = clusters * head_count
    order = ("head", "seq")
    local_slot = cluster_slots(assignment, clusters, capacity)
    slot_ids = jnp.arange(slot_count, dtype=jnp.int32)
    hits = slot_ids[None, :, None] == local_slot.T[:, None, :]
    hits_low = hits.astype(jnp.bfloat16)
    stacked = jnp.stack((query_rows, key_rows, value_rows, grad_rows), axis=2)
    packed = jnp.einsum(
        "hsr,rhaf->hsaf", hits_low, stacked, preferred_element_type=jnp.float32
    ).astype(jnp.bfloat16)
    places = jnp.where(
        jnp.any(hits, axis=2),
        jnp.sum(jnp.where(hits, position.T[:, None, :], 0), axis=2),
        cluster_len,
    ).reshape(devices, capacity)
    coded = jnp.concatenate((places // 32, places % 32), axis=1).astype(jnp.bfloat16)
    coded = jnp.pad(coded, ((0, 0), (0, 2 * head_width - 2 * capacity))).reshape(
        devices, 1, 2, head_width
    )
    payload = jnp.concatenate(
        (packed.reshape(devices, capacity * 2, 2, head_width), coded), axis=1
    )
    rows = 2 * payload.shape[1]
    arrived = lax.all_to_all(payload, order, 0, 0, tiled=True).reshape(devices, rows, head_width)
    arrived_data = arrived[:, : capacity * 4].reshape(devices * capacity, 4 * head_width)
    arrived_code = arrived[:, capacity * 4].astype(jnp.float32)
    flat_place = (
        arrived_code[:, :capacity] * 32.0 + arrived_code[:, capacity : 2 * capacity]
    ).astype(jnp.int32).reshape(-1)
    all_slots = fused_attention(flat_place, arrived_data, cluster_len).reshape(
        devices, capacity, 4, head_width
    )
    returned = lax.all_to_all(all_slots, order, 0, 0, tiled=True).reshape(
        head_count, slot_count, 4 * head_width
    )
    everything = jnp.einsum(
        "hsr,hsf->rhf", hits_low, returned, preferred_element_type=jnp.float32
    ).astype(jnp.bfloat16).reshape(sub_rows, head_count, 4, head_width)
    return (everything[:, :, 0], everything[:, :, 1], everything[:, :, 2], everything[:, :, 3])


def solution(mesh):
    return jax.shard_map(
        shards,
        mesh=mesh,
        in_specs=(
            P(("seq", "head"), None, None),
            P(("seq", "head"), None, None),
            P(("seq", "head"), None, None),
            P(("seq", "head"), None, None),
            P(("seq", "head"), None),
            P(("seq", "head"), None),
        ),
        out_specs=(
            P(("seq", "head"), None, None),
            P(("seq", "head"), None, None),
            P(("seq", "head"), None, None),
            P(("seq", "head"), None, None),
        ),
        check_vma=False,
    )
```

```python
import functools
import math

import jax
import jax.numpy as jnp
from jax import lax
from jax.experimental import pallas as pl
from jax.experimental.pallas import tpu as pltpu
from jax.sharding import PartitionSpec as P


def split_up(x, dim, devices):
    dims = x.shape
    parts = x.reshape(*dims[:dim], devices, dims[dim] // devices, *dims[dim + 1 :])
    return jnp.moveaxis(parts, dim, 0)


def in_order(parts, dim):
    dims = list(parts.shape[1:])
    dims[dim] *= parts.shape[0]
    return jnp.moveaxis(parts, 0, dim).reshape(dims)


def joined_exchange(x, axis, axes, splits, concats):
    sizes = [lax.axis_size(a) for a in axes]
    parts = split_up(x, splits[0], sizes[0])
    parts = jnp.moveaxis(split_up(parts, splits[1] + 1, sizes[1]), 0, 1)
    inside = parts.shape[2:]
    parts = parts.reshape(-1, *inside)
    parts = lax.all_to_all(parts, axis, split_axis=0, concat_axis=0, tiled=True)
    parts = in_order(parts.reshape(*sizes, *inside), concats[0] + 1)
    return in_order(parts, concats[1])


def cluster_slots(assign_cols, clusters, capacity):
    row_count, group_count = assign_cols.shape
    hits = assign_cols[:, :, None] == jnp.arange(clusters, dtype=jnp.int32)[None, None, :]
    onehot = hits.astype(jnp.bfloat16).reshape(row_count, group_count * clusters)
    lower = (
        lax.broadcasted_iota(jnp.int32, (row_count, row_count), 1)
        < lax.broadcasted_iota(jnp.int32, (row_count, row_count), 0)
    ).astype(jnp.bfloat16)
    earlier = jnp.dot(lower, onehot, preferred_element_type=jnp.float32).reshape(
        row_count, group_count, clusters
    )
    within = jnp.sum(jnp.where(hits, earlier, 0.0), axis=2).astype(jnp.int32)
    return assign_cols * capacity + within


def pack_slots(group_rows, group_slot, group_place, slot_count, empty_place):
    slot_ids = jnp.arange(slot_count, dtype=jnp.int32)
    hits = slot_ids[None, :, None] == group_slot[:, None, :]
    packed = jnp.einsum(
        "gsr,grf->gsf", hits.astype(jnp.bfloat16), group_rows, preferred_element_type=jnp.float32
    ).astype(jnp.bfloat16)
    filled = jnp.any(hits, axis=2)
    places = jnp.where(
        filled, jnp.sum(jnp.where(hits, group_place[:, None, :], 0), axis=2), empty_place
    )
    return (packed, places)


def place_tables(flat_place, cluster_len, block_rows):
    tables = []
    for block_index in range(cluster_len // block_rows):
        row_ids = block_index * block_rows + jnp.arange(block_rows, dtype=jnp.int32)
        tables.append((row_ids[:, None] == flat_place[None, :]).astype(jnp.bfloat16))
    return tables


def slots_to_order(tables, arrived_flat):
    return jnp.concatenate(
        [
            jnp.dot(table, arrived_flat, preferred_element_type=jnp.float32).astype(jnp.bfloat16)
            for table in tables
        ],
        axis=0,
    )


def order_to_slots(tables, result_flat, block_rows):
    total = None
    for block_index, table in enumerate(tables):
        piece = result_flat[block_index * block_rows : (block_index + 1) * block_rows]
        term = jnp.einsum("la,lf->af", table, piece, preferred_element_type=jnp.float32)
        total = term if total is None else total + term
    return total.astype(jnp.bfloat16)


def slots_to_rows(returned, local_slot):
    head_count = returned.shape[0]
    flat_rows = returned.reshape(head_count, -1, returned.shape[-1])
    slot_ids = jnp.arange(flat_rows.shape[1], dtype=jnp.int32)
    hits = (local_slot[:, :, None] == slot_ids[None, None, :]).astype(jnp.bfloat16)
    return jnp.einsum("rhs,hsf->rhf", hits, flat_rows, preferred_element_type=jnp.float32).astype(
        jnp.bfloat16
    )


def masked_scores(query_part, key_part, row_start, score_scale):
    scores = (
        jnp.einsum("qd,kd->qk", query_part, key_part, preferred_element_type=jnp.float32)
        * score_scale
    )
    row_ids = row_start + lax.broadcasted_iota(jnp.int32, scores.shape, 0)
    col_ids = lax.broadcasted_iota(jnp.int32, scores.shape, 1)
    return jnp.where(col_ids <= row_ids, scores, -jnp.inf)


def forward_pass(query_block, key_block, value_block, block_rows, score_scale):
    pieces, row_tops, row_totals = ([], [], [])
    for block_index in range(query_block.shape[0] // block_rows):
        row_start = block_index * block_rows
        finish = row_start + block_rows
        scores = masked_scores(
            query_block[row_start:finish], key_block[:finish], row_start, score_scale
        )
        row_top = jnp.max(scores, axis=1, keepdims=True)
        weights = jnp.exp(scores - row_top)
        row_total = jnp.sum(weights, axis=1, keepdims=True)
        probs_low = (weights / row_total).astype(jnp.bfloat16)
        pieces.append(
            jnp.dot(probs_low, value_block[:finish], preferred_element_type=jnp.float32).astype(
                jnp.bfloat16
            )
        )
        row_tops.append(row_top)
        row_totals.append(row_total)
    return (jnp.concatenate(pieces, axis=0), row_tops, row_totals)


def backward_pass(
    query_block,
    key_block,
    value_block,
    grad_block,
    attended_block,
    row_tops,
    row_totals,
    block_rows,
    score_scale,
):
    row_count, head_width = query_block.shape
    grad_key_sum = jnp.zeros((row_count, head_width), jnp.float32)
    grad_value_sum = jnp.zeros((row_count, head_width), jnp.float32)
    query_parts = []
    for block_index in range(row_count // block_rows):
        row_start = block_index * block_rows
        finish = row_start + block_rows
        scores = masked_scores(
            query_block[row_start:finish], key_block[:finish], row_start, score_scale
        )
        probabilities = jnp.exp(scores - row_tops[block_index]) / row_totals[block_index]
        probs_low = probabilities.astype(jnp.bfloat16)
        grad_part = grad_block[row_start:finish]
        grad_prob = jnp.einsum(
            "qd,kd->qk", grad_part, value_block[:finish], preferred_element_type=jnp.float32
        )
        row_delta = jnp.sum(
            grad_part.astype(jnp.float32) * attended_block[row_start:finish].astype(jnp.float32),
            axis=1,
            keepdims=True,
        )
        grad_score = (probabilities * (grad_prob - row_delta)).astype(jnp.bfloat16)
        query_parts.append(
            (
                jnp.dot(grad_score, key_block[:finish], preferred_element_type=jnp.float32)
                * score_scale
            ).astype(jnp.bfloat16)
        )
        key_term = jnp.einsum(
            "qk,qd->kd",
            grad_score,
            query_block[row_start:finish],
            preferred_element_type=jnp.float32,
        )
        value_term = jnp.einsum(
            "qk,qd->kd", probs_low, grad_part, preferred_element_type=jnp.float32
        )
        grad_key_sum = grad_key_sum + jnp.pad(key_term, ((0, row_count - finish), (0, 0)))
        grad_value_sum = grad_value_sum + jnp.pad(value_term, ((0, row_count - finish), (0, 0)))
    grad_query_block = jnp.concatenate(query_parts, axis=0)
    grad_key_block = (grad_key_sum * score_scale).astype(jnp.bfloat16)
    grad_value_block = grad_value_sum.astype(jnp.bfloat16)
    return jnp.stack((grad_query_block, grad_key_block, grad_value_block), axis=1)


def attention_kernel(place_ref, place_col_ref, arrived_ref, out_ref, x_ref, y_ref, dk_acc, dv_acc, *, block_rows):
    rows, width = x_ref.shape
    head_width = width // 4
    scale = 1.0 / math.sqrt(head_width)
    order = (
        lax.broadcasted_iota(jnp.int32, (rows, place_ref.shape[1]), 0) == place_ref[...]
    ).astype(jnp.bfloat16)
    x_ref[...] = jnp.dot(order, arrived_ref[...], preferred_element_type=jnp.float32).astype(
        jnp.bfloat16
    )
    dk_acc[...] = jnp.zeros_like(dk_acc)
    dv_acc[...] = jnp.zeros_like(dv_acc)
    for block_index in range(rows // block_rows):
        start = block_index * block_rows
        finish = start + block_rows
        q_part = x_ref[start:finish, 0:head_width]
        g_part = x_ref[start:finish, 3 * head_width : 4 * head_width]
        k_seen = x_ref[0:finish, head_width : 2 * head_width]
        v_seen = x_ref[0:finish, 2 * head_width : 3 * head_width]
        scores = (
            lax.dot_general(q_part, k_seen, (((1,), (1,)), ((), ())), preferred_element_type=jnp.float32)
            * scale
        )
        row_ids = start + lax.broadcasted_iota(jnp.int32, scores.shape, 0)
        col_ids = lax.broadcasted_iota(jnp.int32, scores.shape, 1)
        scores = jnp.where(col_ids <= row_ids, scores, -jnp.inf)
        row_top = jnp.max(scores, axis=1, keepdims=True)
        weights = jnp.exp(scores - row_top)
        probabilities = weights / jnp.sum(weights, axis=1, keepdims=True)
        probs_low = probabilities.astype(jnp.bfloat16)
        attended = jnp.dot(probs_low, v_seen, preferred_element_type=jnp.float32).astype(jnp.bfloat16)
        y_ref[start:finish, 0:head_width] = attended
        grad_prob = lax.dot_general(
            g_part, v_seen, (((1,), (1,)), ((), ())), preferred_element_type=jnp.float32
        )
        row_delta = jnp.sum(
            g_part.astype(jnp.float32) * attended.astype(jnp.float32), axis=1, keepdims=True
        )
        grad_score = (probabilities * (grad_prob - row_delta)).astype(jnp.bfloat16)
        y_ref[start:finish, head_width : 2 * head_width] = (
            jnp.dot(grad_score, k_seen, preferred_element_type=jnp.float32) * scale
        ).astype(jnp.bfloat16)
        dk_acc[0:finish, :] += lax.dot_general(
            grad_score, q_part, (((0,), (0,)), ((), ())), preferred_element_type=jnp.float32
        )
        dv_acc[0:finish, :] += lax.dot_general(
            probs_low, g_part, (((0,), (0,)), ((), ())), preferred_element_type=jnp.float32
        )
    y_ref[:, 2 * head_width : 3 * head_width] = (dk_acc[...] * scale).astype(jnp.bfloat16)
    y_ref[:, 3 * head_width : 4 * head_width] = dv_acc[...].astype(jnp.bfloat16)
    back = (
        lax.broadcasted_iota(jnp.int32, (place_col_ref.shape[0], rows), 1) == place_col_ref[...]
    ).astype(jnp.bfloat16)
    out_ref[...] = jnp.dot(back, y_ref[...], preferred_element_type=jnp.float32).astype(
        jnp.bfloat16
    )


def fused_attention(flat_place, arrived_flat, cluster_len, block_rows=256):
    slots, width = arrived_flat.shape
    return pl.pallas_call(
        functools.partial(attention_kernel, block_rows=block_rows),
        out_shape=jax.ShapeDtypeStruct((slots, width), jnp.bfloat16),
        scratch_shapes=[
            pltpu.VMEM((cluster_len, width), jnp.bfloat16),
            pltpu.VMEM((cluster_len, width), jnp.bfloat16),
            pltpu.VMEM((cluster_len, width // 4), jnp.float32),
            pltpu.VMEM((cluster_len, width // 4), jnp.float32),
        ],
    )(flat_place.reshape(1, slots), flat_place.reshape(slots, 1), arrived_flat)


def shards(query_rows, key_rows, value_rows, grad_rows, assignment, position):
    sub_rows, head_count, head_width = query_rows.shape
    clusters = lax.axis_size("seq")
    cluster_len = sub_rows * lax.axis_size("head")
    capacity = 3 * sub_rows // (2 * clusters)
    slot_count = clusters * capacity
    devices = clusters * head_count
    order = ("head", "seq")
    local_slot = cluster_slots(assignment, clusters, capacity)
    slot_ids = jnp.arange(slot_count, dtype=jnp.int32)
    hits = slot_ids[None, :, None] == local_slot.T[:, None, :]
    hits_low = hits.astype(jnp.bfloat16)
    stacked = jnp.stack((query_rows, key_rows, value_rows, grad_rows), axis=2)
    packed = jnp.einsum(
        "hsr,rhaf->hsaf", hits_low, stacked, preferred_element_type=jnp.float32
    ).astype(jnp.bfloat16)
    places = jnp.where(
        jnp.any(hits, axis=2),
        jnp.sum(jnp.where(hits, position.T[:, None, :], 0), axis=2),
        cluster_len,
    ).reshape(devices, capacity)
    coded = jnp.concatenate((places // 32, places % 32), axis=1).astype(jnp.bfloat16)
    coded = jnp.pad(coded, ((0, 0), (0, 2 * head_width - 2 * capacity))).reshape(
        devices, 1, 2, head_width
    )
    payload = jnp.concatenate(
        (packed.reshape(devices, capacity * 2, 2, head_width), coded), axis=1
    )
    rows = 2 * payload.shape[1]
    arrived = lax.all_to_all(payload, order, 0, 0, tiled=True).reshape(devices, rows, head_width)
    arrived_data = arrived[:, : capacity * 4].reshape(devices * capacity, 4 * head_width)
    arrived_code = arrived[:, capacity * 4].astype(jnp.float32)
    flat_place = (
        arrived_code[:, :capacity] * 32.0 + arrived_code[:, capacity : 2 * capacity]
    ).astype(jnp.int32).reshape(-1)
    all_slots = fused_attention(flat_place, arrived_data, cluster_len).reshape(
        devices, capacity, 4, head_width
    )
    returned = lax.all_to_all(all_slots, order, 0, 0, tiled=True).reshape(
        head_count, slot_count, 4 * head_width
    )
    everything = jnp.einsum(
        "hsr,hsf->rhf", hits_low, returned, preferred_element_type=jnp.float32
    ).astype(jnp.bfloat16).reshape(sub_rows, head_count, 4, head_width)
    return (everything[:, :, 0], everything[:, :, 1], everything[:, :, 2], everything[:, :, 3])


def solution(mesh):
    return jax.shard_map(
        shards,
        mesh=mesh,
        in_specs=(
            P(("seq", "head"), None, None),
            P(("seq", "head"), None, None),
            P(("seq", "head"), None, None),
            P(("seq", "head"), None, None),
            P(("seq", "head"), None),
            P(("seq", "head"), None),
        ),
        out_specs=(
            P(("seq", "head"), None, None),
            P(("seq", "head"), None, None),
            P(("seq", "head"), None, None),
            P(("seq", "head"), None, None),
        ),
        check_vma=False,
    )
```

```python
import functools
import math

import jax
import jax.numpy as jnp
from jax import lax
from jax.experimental import pallas as pl
from jax.experimental.pallas import tpu as pltpu
from jax.sharding import PartitionSpec as P


def split_up(x, dim, devices):
    dims = x.shape
    parts = x.reshape(*dims[:dim], devices, dims[dim] // devices, *dims[dim + 1 :])
    return jnp.moveaxis(parts, dim, 0)


def in_order(parts, dim):
    dims = list(parts.shape[1:])
    dims[dim] *= parts.shape[0]
    return jnp.moveaxis(parts, 0, dim).reshape(dims)


def joined_exchange(x, axis, axes, splits, concats):
    sizes = [lax.axis_size(a) for a in axes]
    parts = split_up(x, splits[0], sizes[0])
    parts = jnp.moveaxis(split_up(parts, splits[1] + 1, sizes[1]), 0, 1)
    inside = parts.shape[2:]
    parts = parts.reshape(-1, *inside)
    parts = lax.all_to_all(parts, axis, split_axis=0, concat_axis=0, tiled=True)
    parts = in_order(parts.reshape(*sizes, *inside), concats[0] + 1)
    return in_order(parts, concats[1])


def cluster_slots(assign_cols, clusters, capacity):
    row_count, group_count = assign_cols.shape
    hits = assign_cols[:, :, None] == jnp.arange(clusters, dtype=jnp.int32)[None, None, :]
    onehot = hits.astype(jnp.bfloat16).reshape(row_count, group_count * clusters)
    lower = (
        lax.broadcasted_iota(jnp.int32, (row_count, row_count), 1)
        < lax.broadcasted_iota(jnp.int32, (row_count, row_count), 0)
    ).astype(jnp.bfloat16)
    earlier = jnp.dot(lower, onehot, preferred_element_type=jnp.float32).reshape(
        row_count, group_count, clusters
    )
    within = jnp.sum(jnp.where(hits, earlier, 0.0), axis=2).astype(jnp.int32)
    return assign_cols * capacity + within


def pack_slots(group_rows, group_slot, group_place, slot_count, empty_place):
    slot_ids = jnp.arange(slot_count, dtype=jnp.int32)
    hits = slot_ids[None, :, None] == group_slot[:, None, :]
    packed = jnp.einsum(
        "gsr,grf->gsf", hits.astype(jnp.bfloat16), group_rows, preferred_element_type=jnp.float32
    ).astype(jnp.bfloat16)
    filled = jnp.any(hits, axis=2)
    places = jnp.where(
        filled, jnp.sum(jnp.where(hits, group_place[:, None, :], 0), axis=2), empty_place
    )
    return (packed, places)


def place_tables(flat_place, cluster_len, block_rows):
    tables = []
    for block_index in range(cluster_len // block_rows):
        row_ids = block_index * block_rows + jnp.arange(block_rows, dtype=jnp.int32)
        tables.append((row_ids[:, None] == flat_place[None, :]).astype(jnp.bfloat16))
    return tables


def slots_to_order(tables, arrived_flat):
    return jnp.concatenate(
        [
            jnp.dot(table, arrived_flat, preferred_element_type=jnp.float32).astype(jnp.bfloat16)
            for table in tables
        ],
        axis=0,
    )


def order_to_slots(tables, result_flat, block_rows):
    total = None
    for block_index, table in enumerate(tables):
        piece = result_flat[block_index * block_rows : (block_index + 1) * block_rows]
        term = jnp.einsum("la,lf->af", table, piece, preferred_element_type=jnp.float32)
        total = term if total is None else total + term
    return total.astype(jnp.bfloat16)


def slots_to_rows(returned, local_slot):
    head_count = returned.shape[0]
    flat_rows = returned.reshape(head_count, -1, returned.shape[-1])
    slot_ids = jnp.arange(flat_rows.shape[1], dtype=jnp.int32)
    hits = (local_slot[:, :, None] == slot_ids[None, None, :]).astype(jnp.bfloat16)
    return jnp.einsum("rhs,hsf->rhf", hits, flat_rows, preferred_element_type=jnp.float32).astype(
        jnp.bfloat16
    )


def masked_scores(query_part, key_part, row_start, score_scale):
    scores = (
        jnp.einsum("qd,kd->qk", query_part, key_part, preferred_element_type=jnp.float32)
        * score_scale
    )
    row_ids = row_start + lax.broadcasted_iota(jnp.int32, scores.shape, 0)
    col_ids = lax.broadcasted_iota(jnp.int32, scores.shape, 1)
    return jnp.where(col_ids <= row_ids, scores, -jnp.inf)


def forward_pass(query_block, key_block, value_block, block_rows, score_scale):
    pieces, row_tops, row_totals = ([], [], [])
    for block_index in range(query_block.shape[0] // block_rows):
        row_start = block_index * block_rows
        finish = row_start + block_rows
        scores = masked_scores(
            query_block[row_start:finish], key_block[:finish], row_start, score_scale
        )
        row_top = jnp.max(scores, axis=1, keepdims=True)
        weights = jnp.exp(scores - row_top)
        row_total = jnp.sum(weights, axis=1, keepdims=True)
        probs_low = (weights / row_total).astype(jnp.bfloat16)
        pieces.append(
            jnp.dot(probs_low, value_block[:finish], preferred_element_type=jnp.float32).astype(
                jnp.bfloat16
            )
        )
        row_tops.append(row_top)
        row_totals.append(row_total)
    return (jnp.concatenate(pieces, axis=0), row_tops, row_totals)


def backward_pass(
    query_block,
    key_block,
    value_block,
    grad_block,
    attended_block,
    row_tops,
    row_totals,
    block_rows,
    score_scale,
):
    row_count, head_width = query_block.shape
    grad_key_sum = jnp.zeros((row_count, head_width), jnp.float32)
    grad_value_sum = jnp.zeros((row_count, head_width), jnp.float32)
    query_parts = []
    for block_index in range(row_count // block_rows):
        row_start = block_index * block_rows
        finish = row_start + block_rows
        scores = masked_scores(
            query_block[row_start:finish], key_block[:finish], row_start, score_scale
        )
        probabilities = jnp.exp(scores - row_tops[block_index]) / row_totals[block_index]
        probs_low = probabilities.astype(jnp.bfloat16)
        grad_part = grad_block[row_start:finish]
        grad_prob = jnp.einsum(
            "qd,kd->qk", grad_part, value_block[:finish], preferred_element_type=jnp.float32
        )
        row_delta = jnp.sum(
            grad_part.astype(jnp.float32) * attended_block[row_start:finish].astype(jnp.float32),
            axis=1,
            keepdims=True,
        )
        grad_score = (probabilities * (grad_prob - row_delta)).astype(jnp.bfloat16)
        query_parts.append(
            (
                jnp.dot(grad_score, key_block[:finish], preferred_element_type=jnp.float32)
                * score_scale
            ).astype(jnp.bfloat16)
        )
        key_term = jnp.einsum(
            "qk,qd->kd",
            grad_score,
            query_block[row_start:finish],
            preferred_element_type=jnp.float32,
        )
        value_term = jnp.einsum(
            "qk,qd->kd", probs_low, grad_part, preferred_element_type=jnp.float32
        )
        grad_key_sum = grad_key_sum + jnp.pad(key_term, ((0, row_count - finish), (0, 0)))
        grad_value_sum = grad_value_sum + jnp.pad(value_term, ((0, row_count - finish), (0, 0)))
    grad_query_block = jnp.concatenate(query_parts, axis=0)
    grad_key_block = (grad_key_sum * score_scale).astype(jnp.bfloat16)
    grad_value_block = grad_value_sum.astype(jnp.bfloat16)
    return jnp.stack((grad_query_block, grad_key_block, grad_value_block), axis=1)


def attention_kernel(place_ref, arrived_ref, out_ref, x_ref, y_ref, dk_acc, dv_acc, *, block_rows):
    rows, width = x_ref.shape
    head_width = width // 4
    scale = 1.0 / math.sqrt(head_width)
    order = (
        lax.broadcasted_iota(jnp.int32, (rows, place_ref.shape[1]), 0) == place_ref[...]
    ).astype(jnp.bfloat16)
    x_ref[...] = jnp.dot(order, arrived_ref[...], preferred_element_type=jnp.float32).astype(
        jnp.bfloat16
    )
    dk_acc[...] = jnp.zeros_like(dk_acc)
    dv_acc[...] = jnp.zeros_like(dv_acc)
    for block_index in range(rows // block_rows):
        start = block_index * block_rows
        finish = start + block_rows
        q_part = x_ref[start:finish, 0:head_width]
        g_part = x_ref[start:finish, 3 * head_width : 4 * head_width]
        k_seen = x_ref[0:finish, head_width : 2 * head_width]
        v_seen = x_ref[0:finish, 2 * head_width : 3 * head_width]
        scores = (
            lax.dot_general(q_part, k_seen, (((1,), (1,)), ((), ())), preferred_element_type=jnp.float32)
            * scale
        )
        row_ids = start + lax.broadcasted_iota(jnp.int32, scores.shape, 0)
        col_ids = lax.broadcasted_iota(jnp.int32, scores.shape, 1)
        scores = jnp.where(col_ids <= row_ids, scores, -jnp.inf)
        row_top = jnp.max(scores, axis=1, keepdims=True)
        weights = jnp.exp(scores - row_top)
        probabilities = weights / jnp.sum(weights, axis=1, keepdims=True)
        probs_low = probabilities.astype(jnp.bfloat16)
        attended = jnp.dot(probs_low, v_seen, preferred_element_type=jnp.float32).astype(jnp.bfloat16)
        y_ref[start:finish, 0:head_width] = attended
        grad_prob = lax.dot_general(
            g_part, v_seen, (((1,), (1,)), ((), ())), preferred_element_type=jnp.float32
        )
        row_delta = jnp.sum(
            g_part.astype(jnp.float32) * attended.astype(jnp.float32), axis=1, keepdims=True
        )
        grad_score = (probabilities * (grad_prob - row_delta)).astype(jnp.bfloat16)
        y_ref[start:finish, head_width : 2 * head_width] = (
            jnp.dot(grad_score, k_seen, preferred_element_type=jnp.float32) * scale
        ).astype(jnp.bfloat16)
        dk_acc[0:finish, :] += lax.dot_general(
            grad_score, q_part, (((0,), (0,)), ((), ())), preferred_element_type=jnp.float32
        )
        dv_acc[0:finish, :] += lax.dot_general(
            probs_low, g_part, (((0,), (0,)), ((), ())), preferred_element_type=jnp.float32
        )
    y_ref[:, 2 * head_width : 3 * head_width] = (dk_acc[...] * scale).astype(jnp.bfloat16)
    y_ref[:, 3 * head_width : 4 * head_width] = dv_acc[...].astype(jnp.bfloat16)
    out_ref[...] = lax.dot_general(
        order, y_ref[...], (((0,), (0,)), ((), ())), preferred_element_type=jnp.float32
    ).astype(jnp.bfloat16)


def fused_attention(flat_place, arrived_flat, cluster_len, block_rows=512):
    slots, width = arrived_flat.shape
    return pl.pallas_call(
        functools.partial(attention_kernel, block_rows=block_rows),
        out_shape=jax.ShapeDtypeStruct((slots, width), jnp.bfloat16),
        scratch_shapes=[
            pltpu.VMEM((cluster_len, width), jnp.bfloat16),
            pltpu.VMEM((cluster_len, width), jnp.bfloat16),
            pltpu.VMEM((cluster_len, width // 4), jnp.float32),
            pltpu.VMEM((cluster_len, width // 4), jnp.float32),
        ],
    )(flat_place.reshape(1, slots), arrived_flat)


def shards(query_rows, key_rows, value_rows, grad_rows, assignment, position):
    sub_rows, head_count, head_width = query_rows.shape
    clusters = lax.axis_size("seq")
    cluster_len = sub_rows * lax.axis_size("head")
    capacity = 3 * sub_rows // (2 * clusters)
    slot_count = clusters * capacity
    devices = clusters * head_count
    order = ("head", "seq")
    local_slot = cluster_slots(assignment, clusters, capacity)
    slot_ids = jnp.arange(slot_count, dtype=jnp.int32)
    hits = slot_ids[None, :, None] == local_slot.T[:, None, :]
    hits_low = hits.astype(jnp.bfloat16)
    stacked = jnp.stack((query_rows, key_rows, value_rows, grad_rows), axis=2)
    packed = jnp.einsum(
        "hsr,rhaf->hsaf", hits_low, stacked, preferred_element_type=jnp.float32
    ).astype(jnp.bfloat16)
    places = jnp.where(
        jnp.any(hits, axis=2),
        jnp.sum(jnp.where(hits, position.T[:, None, :], 0), axis=2),
        cluster_len,
    ).reshape(devices, capacity)
    coded = jnp.concatenate((places // 32, places % 32), axis=1).astype(jnp.bfloat16)
    coded = jnp.pad(coded, ((0, 0), (0, 2 * head_width - 2 * capacity))).reshape(
        devices, 1, 2, head_width
    )
    payload = jnp.concatenate(
        (packed.reshape(devices, capacity * 2, 2, head_width), coded), axis=1
    )
    rows = 2 * payload.shape[1]
    arrived = lax.all_to_all(payload, order, 0, 0, tiled=True).reshape(devices, rows, head_width)
    arrived_data = arrived[:, : capacity * 4].reshape(devices * capacity, 4 * head_width)
    arrived_code = arrived[:, capacity * 4].astype(jnp.float32)
    flat_place = (
        arrived_code[:, :capacity] * 32.0 + arrived_code[:, capacity : 2 * capacity]
    ).astype(jnp.int32).reshape(-1)
    all_slots = fused_attention(flat_place, arrived_data, cluster_len).reshape(
        devices, capacity, 4, head_width
    )
    returned = lax.all_to_all(all_slots, order, 0, 0, tiled=True).reshape(
        head_count, slot_count, 4 * head_width
    )
    everything = jnp.einsum(
        "hsr,hsf->rhf", hits_low, returned, preferred_element_type=jnp.float32
    ).astype(jnp.bfloat16).reshape(sub_rows, head_count, 4, head_width)
    return (everything[:, :, 0], everything[:, :, 1], everything[:, :, 2], everything[:, :, 3])


def solution(mesh):
    return jax.shard_map(
        shards,
        mesh=mesh,
        in_specs=(
            P(("seq", "head"), None, None),
            P(("seq", "head"), None, None),
            P(("seq", "head"), None, None),
            P(("seq", "head"), None, None),
            P(("seq", "head"), None),
            P(("seq", "head"), None),
        ),
        out_specs=(
            P(("seq", "head"), None, None),
            P(("seq", "head"), None, None),
            P(("seq", "head"), None, None),
            P(("seq", "head"), None, None),
        ),
        check_vma=False,
    )
```

```python
import functools
import math

import jax
import jax.numpy as jnp
from jax import lax
from jax.experimental import pallas as pl
from jax.experimental.pallas import tpu as pltpu
from jax.sharding import PartitionSpec as P


def split_up(x, dim, devices):
    dims = x.shape
    parts = x.reshape(*dims[:dim], devices, dims[dim] // devices, *dims[dim + 1 :])
    return jnp.moveaxis(parts, dim, 0)


def in_order(parts, dim):
    dims = list(parts.shape[1:])
    dims[dim] *= parts.shape[0]
    return jnp.moveaxis(parts, 0, dim).reshape(dims)


def joined_exchange(x, axis, axes, splits, concats):
    sizes = [lax.axis_size(a) for a in axes]
    parts = split_up(x, splits[0], sizes[0])
    parts = jnp.moveaxis(split_up(parts, splits[1] + 1, sizes[1]), 0, 1)
    inside = parts.shape[2:]
    parts = parts.reshape(-1, *inside)
    parts = lax.all_to_all(parts, axis, split_axis=0, concat_axis=0, tiled=True)
    parts = in_order(parts.reshape(*sizes, *inside), concats[0] + 1)
    return in_order(parts, concats[1])


def cluster_slots(assign_cols, clusters, capacity):
    row_count, group_count = assign_cols.shape
    hits = assign_cols[:, :, None] == jnp.arange(clusters, dtype=jnp.int32)[None, None, :]
    onehot = hits.astype(jnp.bfloat16).reshape(row_count, group_count * clusters)
    lower = (
        lax.broadcasted_iota(jnp.int32, (row_count, row_count), 1)
        < lax.broadcasted_iota(jnp.int32, (row_count, row_count), 0)
    ).astype(jnp.bfloat16)
    earlier = jnp.dot(lower, onehot, preferred_element_type=jnp.float32).reshape(
        row_count, group_count, clusters
    )
    within = jnp.sum(jnp.where(hits, earlier, 0.0), axis=2).astype(jnp.int32)
    return assign_cols * capacity + within


def pack_slots(group_rows, group_slot, group_place, slot_count, empty_place):
    slot_ids = jnp.arange(slot_count, dtype=jnp.int32)
    hits = slot_ids[None, :, None] == group_slot[:, None, :]
    packed = jnp.einsum(
        "gsr,grf->gsf", hits.astype(jnp.bfloat16), group_rows, preferred_element_type=jnp.float32
    ).astype(jnp.bfloat16)
    filled = jnp.any(hits, axis=2)
    places = jnp.where(
        filled, jnp.sum(jnp.where(hits, group_place[:, None, :], 0), axis=2), empty_place
    )
    return (packed, places)


def place_tables(flat_place, cluster_len, block_rows):
    tables = []
    for block_index in range(cluster_len // block_rows):
        row_ids = block_index * block_rows + jnp.arange(block_rows, dtype=jnp.int32)
        tables.append((row_ids[:, None] == flat_place[None, :]).astype(jnp.bfloat16))
    return tables


def slots_to_order(tables, arrived_flat):
    return jnp.concatenate(
        [
            jnp.dot(table, arrived_flat, preferred_element_type=jnp.float32).astype(jnp.bfloat16)
            for table in tables
        ],
        axis=0,
    )


def order_to_slots(tables, result_flat, block_rows):
    total = None
    for block_index, table in enumerate(tables):
        piece = result_flat[block_index * block_rows : (block_index + 1) * block_rows]
        term = jnp.einsum("la,lf->af", table, piece, preferred_element_type=jnp.float32)
        total = term if total is None else total + term
    return total.astype(jnp.bfloat16)


def slots_to_rows(returned, local_slot):
    head_count = returned.shape[0]
    flat_rows = returned.reshape(head_count, -1, returned.shape[-1])
    slot_ids = jnp.arange(flat_rows.shape[1], dtype=jnp.int32)
    hits = (local_slot[:, :, None] == slot_ids[None, None, :]).astype(jnp.bfloat16)
    return jnp.einsum("rhs,hsf->rhf", hits, flat_rows, preferred_element_type=jnp.float32).astype(
        jnp.bfloat16
    )


def masked_scores(query_part, key_part, row_start, score_scale):
    scores = (
        jnp.einsum("qd,kd->qk", query_part, key_part, preferred_element_type=jnp.float32)
        * score_scale
    )
    row_ids = row_start + lax.broadcasted_iota(jnp.int32, scores.shape, 0)
    col_ids = lax.broadcasted_iota(jnp.int32, scores.shape, 1)
    return jnp.where(col_ids <= row_ids, scores, -jnp.inf)


def forward_pass(query_block, key_block, value_block, block_rows, score_scale):
    pieces, row_tops, row_totals = ([], [], [])
    for block_index in range(query_block.shape[0] // block_rows):
        row_start = block_index * block_rows
        finish = row_start + block_rows
        scores = masked_scores(
            query_block[row_start:finish], key_block[:finish], row_start, score_scale
        )
        row_top = jnp.max(scores, axis=1, keepdims=True)
        weights = jnp.exp(scores - row_top)
        row_total = jnp.sum(weights, axis=1, keepdims=True)
        probs_low = (weights / row_total).astype(jnp.bfloat16)
        pieces.append(
            jnp.dot(probs_low, value_block[:finish], preferred_element_type=jnp.float32).astype(
                jnp.bfloat16
            )
        )
        row_tops.append(row_top)
        row_totals.append(row_total)
    return (jnp.concatenate(pieces, axis=0), row_tops, row_totals)


def backward_pass(
    query_block,
    key_block,
    value_block,
    grad_block,
    attended_block,
    row_tops,
    row_totals,
    block_rows,
    score_scale,
):
    row_count, head_width = query_block.shape
    grad_key_sum = jnp.zeros((row_count, head_width), jnp.float32)
    grad_value_sum = jnp.zeros((row_count, head_width), jnp.float32)
    query_parts = []
    for block_index in range(row_count // block_rows):
        row_start = block_index * block_rows
        finish = row_start + block_rows
        scores = masked_scores(
            query_block[row_start:finish], key_block[:finish], row_start, score_scale
        )
        probabilities = jnp.exp(scores - row_tops[block_index]) / row_totals[block_index]
        probs_low = probabilities.astype(jnp.bfloat16)
        grad_part = grad_block[row_start:finish]
        grad_prob = jnp.einsum(
            "qd,kd->qk", grad_part, value_block[:finish], preferred_element_type=jnp.float32
        )
        row_delta = jnp.sum(
            grad_part.astype(jnp.float32) * attended_block[row_start:finish].astype(jnp.float32),
            axis=1,
            keepdims=True,
        )
        grad_score = (probabilities * (grad_prob - row_delta)).astype(jnp.bfloat16)
        query_parts.append(
            (
                jnp.dot(grad_score, key_block[:finish], preferred_element_type=jnp.float32)
                * score_scale
            ).astype(jnp.bfloat16)
        )
        key_term = jnp.einsum(
            "qk,qd->kd",
            grad_score,
            query_block[row_start:finish],
            preferred_element_type=jnp.float32,
        )
        value_term = jnp.einsum(
            "qk,qd->kd", probs_low, grad_part, preferred_element_type=jnp.float32
        )
        grad_key_sum = grad_key_sum + jnp.pad(key_term, ((0, row_count - finish), (0, 0)))
        grad_value_sum = grad_value_sum + jnp.pad(value_term, ((0, row_count - finish), (0, 0)))
    grad_query_block = jnp.concatenate(query_parts, axis=0)
    grad_key_block = (grad_key_sum * score_scale).astype(jnp.bfloat16)
    grad_value_block = grad_value_sum.astype(jnp.bfloat16)
    return jnp.stack((grad_query_block, grad_key_block, grad_value_block), axis=1)


def attention_kernel(place_ref, arrived_ref, out_ref, x_ref, y_ref, dk_acc, dv_acc, *, block_rows):
    rows, width = x_ref.shape
    head_width = width // 4
    scale = 1.0 / math.sqrt(head_width)
    order = (
        lax.broadcasted_iota(jnp.int32, (rows, place_ref.shape[1]), 0) == place_ref[...]
    ).astype(jnp.bfloat16)
    x_ref[...] = jnp.dot(order, arrived_ref[...], preferred_element_type=jnp.float32).astype(
        jnp.bfloat16
    )
    dk_acc[...] = jnp.zeros_like(dk_acc)
    dv_acc[...] = jnp.zeros_like(dv_acc)
    for block_index in range(rows // block_rows):
        start = block_index * block_rows
        finish = start + block_rows
        q_part = x_ref[start:finish, 0:head_width]
        g_part = x_ref[start:finish, 3 * head_width : 4 * head_width]
        k_seen = x_ref[0:finish, head_width : 2 * head_width]
        v_seen = x_ref[0:finish, 2 * head_width : 3 * head_width]
        scores = (
            lax.dot_general(q_part, k_seen, (((1,), (1,)), ((), ())), preferred_element_type=jnp.float32)
            * scale
        )
        row_ids = start + lax.broadcasted_iota(jnp.int32, scores.shape, 0)
        col_ids = lax.broadcasted_iota(jnp.int32, scores.shape, 1)
        scores = jnp.where(col_ids <= row_ids, scores, -jnp.inf)
        row_top = jnp.max(scores, axis=1, keepdims=True)
        weights = jnp.exp(scores - row_top)
        probabilities = weights / jnp.sum(weights, axis=1, keepdims=True)
        probs_low = probabilities.astype(jnp.bfloat16)
        attended = jnp.dot(probs_low, v_seen, preferred_element_type=jnp.float32).astype(jnp.bfloat16)
        y_ref[start:finish, 0:head_width] = attended
        grad_prob = lax.dot_general(
            g_part, v_seen, (((1,), (1,)), ((), ())), preferred_element_type=jnp.float32
        )
        row_delta = jnp.sum(
            g_part.astype(jnp.float32) * attended.astype(jnp.float32), axis=1, keepdims=True
        )
        grad_score = (probabilities * (grad_prob - row_delta)).astype(jnp.bfloat16)
        y_ref[start:finish, head_width : 2 * head_width] = (
            jnp.dot(grad_score, k_seen, preferred_element_type=jnp.float32) * scale
        ).astype(jnp.bfloat16)
        dk_acc[0:finish, :] += lax.dot_general(
            grad_score, q_part, (((0,), (0,)), ((), ())), preferred_element_type=jnp.float32
        )
        dv_acc[0:finish, :] += lax.dot_general(
            probs_low, g_part, (((0,), (0,)), ((), ())), preferred_element_type=jnp.float32
        )
    y_ref[:, 2 * head_width : 3 * head_width] = (dk_acc[...] * scale).astype(jnp.bfloat16)
    y_ref[:, 3 * head_width : 4 * head_width] = dv_acc[...].astype(jnp.bfloat16)
    out_ref[...] = lax.dot_general(
        order, y_ref[...], (((0,), (0,)), ((), ())), preferred_element_type=jnp.float32
    ).astype(jnp.bfloat16)


def fused_attention(flat_place, arrived_flat, cluster_len, block_rows=256):
    slots, width = arrived_flat.shape
    return pl.pallas_call(
        functools.partial(attention_kernel, block_rows=block_rows),
        out_shape=jax.ShapeDtypeStruct((slots, width), jnp.bfloat16),
        scratch_shapes=[
            pltpu.VMEM((cluster_len, width), jnp.bfloat16),
            pltpu.VMEM((cluster_len, width), jnp.bfloat16),
            pltpu.VMEM((cluster_len, width // 4), jnp.float32),
            pltpu.VMEM((cluster_len, width // 4), jnp.float32),
        ],
    )(flat_place.reshape(1, slots), arrived_flat)


def shards(query_rows, key_rows, value_rows, grad_rows, assignment, position):
    sub_rows, head_count, head_width = query_rows.shape
    clusters = lax.axis_size("seq")
    cluster_len = sub_rows * lax.axis_size("head")
    capacity = 3 * sub_rows // (2 * clusters)
    slot_count = clusters * capacity
    devices = clusters * head_count
    order = ("head", "seq")
    local_slot = cluster_slots(assignment, clusters, capacity)
    slot_ids = jnp.arange(slot_count, dtype=jnp.int32)
    hits = slot_ids[None, :, None] == local_slot.T[:, None, :]
    hits_low = hits.astype(jnp.bfloat16)
    stacked = jnp.stack((query_rows, key_rows, value_rows, grad_rows), axis=2)
    packed = jnp.einsum(
        "hsr,rhaf->hsaf", hits_low, stacked, preferred_element_type=jnp.float32
    ).astype(jnp.bfloat16)
    places = jnp.where(
        jnp.any(hits, axis=2),
        jnp.sum(jnp.where(hits, position.T[:, None, :], 0), axis=2),
        cluster_len,
    ).reshape(devices, capacity)
    coded = jnp.concatenate((places // 32, places % 32), axis=1).astype(jnp.bfloat16)
    coded = jnp.pad(coded, ((0, 0), (0, 2 * head_width - 2 * capacity))).reshape(
        devices, 1, 2, head_width
    )
    payload = jnp.concatenate(
        (packed.reshape(devices, capacity * 2, 2, head_width), coded), axis=1
    )
    rows = 2 * payload.shape[1]
    arrived = lax.all_to_all(payload, order, 0, 0, tiled=True).reshape(devices, rows, head_width)
    arrived_data = arrived[:, : capacity * 4].reshape(devices * capacity, 4 * head_width)
    arrived_code = arrived[:, capacity * 4].astype(jnp.float32)
    flat_place = (
        arrived_code[:, :capacity] * 32.0 + arrived_code[:, capacity : 2 * capacity]
    ).astype(jnp.int32).reshape(-1)
    all_slots = fused_attention(flat_place, arrived_data, cluster_len).reshape(
        devices, capacity, 4, head_width
    )
    returned = lax.all_to_all(all_slots, order, 0, 0, tiled=True).reshape(
        devices * capacity, 4 * head_width
    )
    back_target = (jnp.arange(head_count, dtype=jnp.int32)[None, :] * slot_count + local_slot).reshape(-1)
    back_hits = (
        jnp.arange(devices * capacity, dtype=jnp.int32)[None, :] == back_target[:, None]
    ).astype(jnp.bfloat16)
    everything = jnp.dot(back_hits, returned, preferred_element_type=jnp.float32)
    return tuple(
        everything[:, member * head_width : (member + 1) * head_width]
        .astype(jnp.bfloat16)
        .reshape(sub_rows, head_count, head_width)
        for member in range(4)
    )


def solution(mesh):
    return jax.shard_map(
        shards,
        mesh=mesh,
        in_specs=(
            P(("seq", "head"), None, None),
            P(("seq", "head"), None, None),
            P(("seq", "head"), None, None),
            P(("seq", "head"), None, None),
            P(("seq", "head"), None),
            P(("seq", "head"), None),
        ),
        out_specs=(
            P(("seq", "head"), None, None),
            P(("seq", "head"), None, None),
            P(("seq", "head"), None, None),
            P(("seq", "head"), None, None),
        ),
        check_vma=False,
    )
```

```python
import functools
import math

import jax
import jax.numpy as jnp
from jax import lax
from jax.experimental import pallas as pl
from jax.experimental.pallas import tpu as pltpu
from jax.sharding import PartitionSpec as P


def split_up(x, dim, devices):
    dims = x.shape
    parts = x.reshape(*dims[:dim], devices, dims[dim] // devices, *dims[dim + 1 :])
    return jnp.moveaxis(parts, dim, 0)


def in_order(parts, dim):
    dims = list(parts.shape[1:])
    dims[dim] *= parts.shape[0]
    return jnp.moveaxis(parts, 0, dim).reshape(dims)


def joined_exchange(x, axis, axes, splits, concats):
    sizes = [lax.axis_size(a) for a in axes]
    parts = split_up(x, splits[0], sizes[0])
    parts = jnp.moveaxis(split_up(parts, splits[1] + 1, sizes[1]), 0, 1)
    inside = parts.shape[2:]
    parts = parts.reshape(-1, *inside)
    parts = lax.all_to_all(parts, axis, split_axis=0, concat_axis=0, tiled=True)
    parts = in_order(parts.reshape(*sizes, *inside), concats[0] + 1)
    return in_order(parts, concats[1])


def cluster_slots(assign_cols, clusters, capacity):
    row_count, group_count = assign_cols.shape
    hits = assign_cols[:, :, None] == jnp.arange(clusters, dtype=jnp.int32)[None, None, :]
    onehot = hits.astype(jnp.bfloat16).reshape(row_count, group_count * clusters)
    lower = (
        lax.broadcasted_iota(jnp.int32, (row_count, row_count), 1)
        < lax.broadcasted_iota(jnp.int32, (row_count, row_count), 0)
    ).astype(jnp.bfloat16)
    earlier = jnp.dot(lower, onehot, preferred_element_type=jnp.float32).reshape(
        row_count, group_count, clusters
    )
    within = jnp.sum(jnp.where(hits, earlier, 0.0), axis=2).astype(jnp.int32)
    return assign_cols * capacity + within


def pack_slots(group_rows, group_slot, group_place, slot_count, empty_place):
    slot_ids = jnp.arange(slot_count, dtype=jnp.int32)
    hits = slot_ids[None, :, None] == group_slot[:, None, :]
    packed = jnp.einsum(
        "gsr,grf->gsf", hits.astype(jnp.bfloat16), group_rows, preferred_element_type=jnp.float32
    ).astype(jnp.bfloat16)
    filled = jnp.any(hits, axis=2)
    places = jnp.where(
        filled, jnp.sum(jnp.where(hits, group_place[:, None, :], 0), axis=2), empty_place
    )
    return (packed, places)


def place_tables(flat_place, cluster_len, block_rows):
    tables = []
    for block_index in range(cluster_len // block_rows):
        row_ids = block_index * block_rows + jnp.arange(block_rows, dtype=jnp.int32)
        tables.append((row_ids[:, None] == flat_place[None, :]).astype(jnp.bfloat16))
    return tables


def slots_to_order(tables, arrived_flat):
    return jnp.concatenate(
        [
            jnp.dot(table, arrived_flat, preferred_element_type=jnp.float32).astype(jnp.bfloat16)
            for table in tables
        ],
        axis=0,
    )


def order_to_slots(tables, result_flat, block_rows):
    total = None
    for block_index, table in enumerate(tables):
        piece = result_flat[block_index * block_rows : (block_index + 1) * block_rows]
        term = jnp.einsum("la,lf->af", table, piece, preferred_element_type=jnp.float32)
        total = term if total is None else total + term
    return total.astype(jnp.bfloat16)


def slots_to_rows(returned, local_slot):
    head_count = returned.shape[0]
    flat_rows = returned.reshape(head_count, -1, returned.shape[-1])
    slot_ids = jnp.arange(flat_rows.shape[1], dtype=jnp.int32)
    hits = (local_slot[:, :, None] == slot_ids[None, None, :]).astype(jnp.bfloat16)
    return jnp.einsum("rhs,hsf->rhf", hits, flat_rows, preferred_element_type=jnp.float32).astype(
        jnp.bfloat16
    )


def masked_scores(query_part, key_part, row_start, score_scale):
    scores = (
        jnp.einsum("qd,kd->qk", query_part, key_part, preferred_element_type=jnp.float32)
        * score_scale
    )
    row_ids = row_start + lax.broadcasted_iota(jnp.int32, scores.shape, 0)
    col_ids = lax.broadcasted_iota(jnp.int32, scores.shape, 1)
    return jnp.where(col_ids <= row_ids, scores, -jnp.inf)


def forward_pass(query_block, key_block, value_block, block_rows, score_scale):
    pieces, row_tops, row_totals = ([], [], [])
    for block_index in range(query_block.shape[0] // block_rows):
        row_start = block_index * block_rows
        finish = row_start + block_rows
        scores = masked_scores(
            query_block[row_start:finish], key_block[:finish], row_start, score_scale
        )
        row_top = jnp.max(scores, axis=1, keepdims=True)
        weights = jnp.exp(scores - row_top)
        row_total = jnp.sum(weights, axis=1, keepdims=True)
        probs_low = (weights / row_total).astype(jnp.bfloat16)
        pieces.append(
            jnp.dot(probs_low, value_block[:finish], preferred_element_type=jnp.float32).astype(
                jnp.bfloat16
            )
        )
        row_tops.append(row_top)
        row_totals.append(row_total)
    return (jnp.concatenate(pieces, axis=0), row_tops, row_totals)


def backward_pass(
    query_block,
    key_block,
    value_block,
    grad_block,
    attended_block,
    row_tops,
    row_totals,
    block_rows,
    score_scale,
):
    row_count, head_width = query_block.shape
    grad_key_sum = jnp.zeros((row_count, head_width), jnp.float32)
    grad_value_sum = jnp.zeros((row_count, head_width), jnp.float32)
    query_parts = []
    for block_index in range(row_count // block_rows):
        row_start = block_index * block_rows
        finish = row_start + block_rows
        scores = masked_scores(
            query_block[row_start:finish], key_block[:finish], row_start, score_scale
        )
        probabilities = jnp.exp(scores - row_tops[block_index]) / row_totals[block_index]
        probs_low = probabilities.astype(jnp.bfloat16)
        grad_part = grad_block[row_start:finish]
        grad_prob = jnp.einsum(
            "qd,kd->qk", grad_part, value_block[:finish], preferred_element_type=jnp.float32
        )
        row_delta = jnp.sum(
            grad_part.astype(jnp.float32) * attended_block[row_start:finish].astype(jnp.float32),
            axis=1,
            keepdims=True,
        )
        grad_score = (probabilities * (grad_prob - row_delta)).astype(jnp.bfloat16)
        query_parts.append(
            (
                jnp.dot(grad_score, key_block[:finish], preferred_element_type=jnp.float32)
                * score_scale
            ).astype(jnp.bfloat16)
        )
        key_term = jnp.einsum(
            "qk,qd->kd",
            grad_score,
            query_block[row_start:finish],
            preferred_element_type=jnp.float32,
        )
        value_term = jnp.einsum(
            "qk,qd->kd", probs_low, grad_part, preferred_element_type=jnp.float32
        )
        grad_key_sum = grad_key_sum + jnp.pad(key_term, ((0, row_count - finish), (0, 0)))
        grad_value_sum = grad_value_sum + jnp.pad(value_term, ((0, row_count - finish), (0, 0)))
    grad_query_block = jnp.concatenate(query_parts, axis=0)
    grad_key_block = (grad_key_sum * score_scale).astype(jnp.bfloat16)
    grad_value_block = grad_value_sum.astype(jnp.bfloat16)
    return jnp.stack((grad_query_block, grad_key_block, grad_value_block), axis=1)


def attention_kernel(place_ref, arrived_ref, out_ref, x_ref, y_ref, dk_acc, dv_acc, *, block_rows):
    rows, width = x_ref.shape
    head_width = width // 4
    scale = 1.0 / math.sqrt(head_width)
    order = (
        lax.broadcasted_iota(jnp.int32, (rows, place_ref.shape[1]), 0) == place_ref[...]
    ).astype(jnp.bfloat16)
    x_ref[...] = jnp.dot(order, arrived_ref[...], preferred_element_type=jnp.float32).astype(
        jnp.bfloat16
    )
    dk_acc[...] = jnp.zeros_like(dk_acc)
    dv_acc[...] = jnp.zeros_like(dv_acc)
    for block_index in range(rows // block_rows):
        start = block_index * block_rows
        finish = start + block_rows
        q_part = x_ref[start:finish, 0:head_width]
        g_part = x_ref[start:finish, 3 * head_width : 4 * head_width]
        k_seen = x_ref[0:finish, head_width : 2 * head_width]
        v_seen = x_ref[0:finish, 2 * head_width : 3 * head_width]
        scores = (
            lax.dot_general(q_part, k_seen, (((1,), (1,)), ((), ())), preferred_element_type=jnp.float32)
            * scale
        )
        row_ids = start + lax.broadcasted_iota(jnp.int32, scores.shape, 0)
        col_ids = lax.broadcasted_iota(jnp.int32, scores.shape, 1)
        scores = jnp.where(col_ids <= row_ids, scores, -jnp.inf)
        row_top = jnp.max(scores, axis=1, keepdims=True)
        weights = jnp.exp(scores - row_top)
        probabilities = weights / jnp.sum(weights, axis=1, keepdims=True)
        probs_low = probabilities.astype(jnp.bfloat16)
        attended = jnp.dot(probs_low, v_seen, preferred_element_type=jnp.float32).astype(jnp.bfloat16)
        y_ref[start:finish, 0:head_width] = attended
        grad_prob = lax.dot_general(
            g_part, v_seen, (((1,), (1,)), ((), ())), preferred_element_type=jnp.float32
        )
        row_delta = jnp.sum(
            g_part.astype(jnp.float32) * attended.astype(jnp.float32), axis=1, keepdims=True
        )
        grad_score = (probabilities * (grad_prob - row_delta)).astype(jnp.bfloat16)
        y_ref[start:finish, head_width : 2 * head_width] = (
            jnp.dot(grad_score, k_seen, preferred_element_type=jnp.float32) * scale
        ).astype(jnp.bfloat16)
        dk_acc[0:finish, :] += lax.dot_general(
            grad_score, q_part, (((0,), (0,)), ((), ())), preferred_element_type=jnp.float32
        )
        dv_acc[0:finish, :] += lax.dot_general(
            probs_low, g_part, (((0,), (0,)), ((), ())), preferred_element_type=jnp.float32
        )
    y_ref[:, 2 * head_width : 3 * head_width] = (dk_acc[...] * scale).astype(jnp.bfloat16)
    y_ref[:, 3 * head_width : 4 * head_width] = dv_acc[...].astype(jnp.bfloat16)
    result = lax.dot_general(
        order, y_ref[...], (((0,), (0,)), ((), ())), preferred_element_type=jnp.float32
    )
    for member in range(4):
        out_ref[pl.ds(member, place_ref.shape[1], stride=4), :] = result[
            :, member * head_width : (member + 1) * head_width
        ]


def fused_attention(flat_place, arrived_flat, cluster_len, block_rows=256):
    slots, width = arrived_flat.shape
    return pl.pallas_call(
        functools.partial(attention_kernel, block_rows=block_rows),
        out_shape=jax.ShapeDtypeStruct((slots * 4, width // 4), jnp.float32),
        scratch_shapes=[
            pltpu.VMEM((cluster_len, width), jnp.bfloat16),
            pltpu.VMEM((cluster_len, width), jnp.bfloat16),
            pltpu.VMEM((cluster_len, width // 4), jnp.float32),
            pltpu.VMEM((cluster_len, width // 4), jnp.float32),
        ],
    )(flat_place.reshape(1, slots), arrived_flat)


def shards(query_rows, key_rows, value_rows, grad_rows, assignment, position):
    sub_rows, head_count, head_width = query_rows.shape
    clusters = lax.axis_size("seq")
    cluster_len = sub_rows * lax.axis_size("head")
    capacity = 3 * sub_rows // (2 * clusters)
    slot_count = clusters * capacity
    devices = clusters * head_count
    order = ("head", "seq")
    local_slot = cluster_slots(assignment, clusters, capacity)
    slot_ids = jnp.arange(slot_count, dtype=jnp.int32)
    hits = slot_ids[None, :, None] == local_slot.T[:, None, :]
    hits_low = hits.astype(jnp.bfloat16)
    stacked = jnp.stack((query_rows, key_rows, value_rows, grad_rows), axis=2)
    packed = jnp.einsum(
        "hsr,rhaf->hsaf", hits_low, stacked, preferred_element_type=jnp.float32
    ).astype(jnp.bfloat16)
    places = jnp.where(
        jnp.any(hits, axis=2),
        jnp.sum(jnp.where(hits, position.T[:, None, :], 0), axis=2),
        cluster_len,
    ).reshape(devices, capacity)
    coded = jnp.concatenate((places // 32, places % 32), axis=1).astype(jnp.bfloat16)
    coded = jnp.pad(coded, ((0, 0), (0, 2 * head_width - 2 * capacity))).reshape(
        devices, 1, 2, head_width
    )
    payload = jnp.concatenate(
        (packed.reshape(devices, capacity * 2, 2, head_width), coded), axis=1
    )
    rows = 2 * payload.shape[1]
    arrived = lax.all_to_all(payload, order, 0, 0, tiled=True).reshape(devices, rows, head_width)
    arrived_data = arrived[:, : capacity * 4].reshape(devices * capacity, 4 * head_width)
    arrived_code = arrived[:, capacity * 4].astype(jnp.float32)
    flat_place = (
        arrived_code[:, :capacity] * 32.0 + arrived_code[:, capacity : 2 * capacity]
    ).astype(jnp.int32).reshape(-1)
    all_slots = (
        fused_attention(flat_place, arrived_data, cluster_len)
        .astype(jnp.bfloat16)
        .reshape(devices, capacity, 4, head_width)
    )
    returned = lax.all_to_all(all_slots, order, 0, 0, tiled=True).reshape(
        devices * capacity, 4 * head_width
    )
    back_target = (jnp.arange(head_count, dtype=jnp.int32)[None, :] * slot_count + local_slot).reshape(-1)
    back_hits = (
        jnp.arange(devices * capacity, dtype=jnp.int32)[None, :] == back_target[:, None]
    ).astype(jnp.bfloat16)
    everything = jnp.dot(back_hits, returned, preferred_element_type=jnp.float32)
    return tuple(
        everything[:, member * head_width : (member + 1) * head_width]
        .astype(jnp.bfloat16)
        .reshape(sub_rows, head_count, head_width)
        for member in range(4)
    )


def solution(mesh):
    return jax.shard_map(
        shards,
        mesh=mesh,
        in_specs=(
            P(("seq", "head"), None, None),
            P(("seq", "head"), None, None),
            P(("seq", "head"), None, None),
            P(("seq", "head"), None, None),
            P(("seq", "head"), None),
            P(("seq", "head"), None),
        ),
        out_specs=(
            P(("seq", "head"), None, None),
            P(("seq", "head"), None, None),
            P(("seq", "head"), None, None),
            P(("seq", "head"), None, None),
        ),
        check_vma=False,
    )
```

```python
import functools
import math

import jax
import jax.numpy as jnp
from jax import lax
from jax.experimental import pallas as pl
from jax.experimental.pallas import tpu as pltpu
from jax.sharding import PartitionSpec as P


def split_up(x, dim, devices):
    dims = x.shape
    parts = x.reshape(*dims[:dim], devices, dims[dim] // devices, *dims[dim + 1 :])
    return jnp.moveaxis(parts, dim, 0)


def in_order(parts, dim):
    dims = list(parts.shape[1:])
    dims[dim] *= parts.shape[0]
    return jnp.moveaxis(parts, 0, dim).reshape(dims)


def joined_exchange(x, axis, axes, splits, concats):
    sizes = [lax.axis_size(a) for a in axes]
    parts = split_up(x, splits[0], sizes[0])
    parts = jnp.moveaxis(split_up(parts, splits[1] + 1, sizes[1]), 0, 1)
    inside = parts.shape[2:]
    parts = parts.reshape(-1, *inside)
    parts = lax.all_to_all(parts, axis, split_axis=0, concat_axis=0, tiled=True)
    parts = in_order(parts.reshape(*sizes, *inside), concats[0] + 1)
    return in_order(parts, concats[1])


def cluster_slots(assign_cols, clusters, capacity):
    row_count, group_count = assign_cols.shape
    hits = assign_cols[:, :, None] == jnp.arange(clusters, dtype=jnp.int32)[None, None, :]
    onehot = hits.astype(jnp.bfloat16).reshape(row_count, group_count * clusters)
    lower = (
        lax.broadcasted_iota(jnp.int32, (row_count, row_count), 1)
        < lax.broadcasted_iota(jnp.int32, (row_count, row_count), 0)
    ).astype(jnp.bfloat16)
    earlier = jnp.dot(lower, onehot, preferred_element_type=jnp.float32).reshape(
        row_count, group_count, clusters
    )
    within = jnp.sum(jnp.where(hits, earlier, 0.0), axis=2).astype(jnp.int32)
    return assign_cols * capacity + within


def pack_slots(group_rows, group_slot, group_place, slot_count, empty_place):
    slot_ids = jnp.arange(slot_count, dtype=jnp.int32)
    hits = slot_ids[None, :, None] == group_slot[:, None, :]
    packed = jnp.einsum(
        "gsr,grf->gsf", hits.astype(jnp.bfloat16), group_rows, preferred_element_type=jnp.float32
    ).astype(jnp.bfloat16)
    filled = jnp.any(hits, axis=2)
    places = jnp.where(
        filled, jnp.sum(jnp.where(hits, group_place[:, None, :], 0), axis=2), empty_place
    )
    return (packed, places)


def place_tables(flat_place, cluster_len, block_rows):
    tables = []
    for block_index in range(cluster_len // block_rows):
        row_ids = block_index * block_rows + jnp.arange(block_rows, dtype=jnp.int32)
        tables.append((row_ids[:, None] == flat_place[None, :]).astype(jnp.bfloat16))
    return tables


def slots_to_order(tables, arrived_flat):
    return jnp.concatenate(
        [
            jnp.dot(table, arrived_flat, preferred_element_type=jnp.float32).astype(jnp.bfloat16)
            for table in tables
        ],
        axis=0,
    )


def order_to_slots(tables, result_flat, block_rows):
    total = None
    for block_index, table in enumerate(tables):
        piece = result_flat[block_index * block_rows : (block_index + 1) * block_rows]
        term = jnp.einsum("la,lf->af", table, piece, preferred_element_type=jnp.float32)
        total = term if total is None else total + term
    return total.astype(jnp.bfloat16)


def slots_to_rows(returned, local_slot):
    head_count = returned.shape[0]
    flat_rows = returned.reshape(head_count, -1, returned.shape[-1])
    slot_ids = jnp.arange(flat_rows.shape[1], dtype=jnp.int32)
    hits = (local_slot[:, :, None] == slot_ids[None, None, :]).astype(jnp.bfloat16)
    return jnp.einsum("rhs,hsf->rhf", hits, flat_rows, preferred_element_type=jnp.float32).astype(
        jnp.bfloat16
    )


def masked_scores(query_part, key_part, row_start, score_scale):
    scores = (
        jnp.einsum("qd,kd->qk", query_part, key_part, preferred_element_type=jnp.float32)
        * score_scale
    )
    row_ids = row_start + lax.broadcasted_iota(jnp.int32, scores.shape, 0)
    col_ids = lax.broadcasted_iota(jnp.int32, scores.shape, 1)
    return jnp.where(col_ids <= row_ids, scores, -jnp.inf)


def forward_pass(query_block, key_block, value_block, block_rows, score_scale):
    pieces, row_tops, row_totals = ([], [], [])
    for block_index in range(query_block.shape[0] // block_rows):
        row_start = block_index * block_rows
        finish = row_start + block_rows
        scores = masked_scores(
            query_block[row_start:finish], key_block[:finish], row_start, score_scale
        )
        row_top = jnp.max(scores, axis=1, keepdims=True)
        weights = jnp.exp(scores - row_top)
        row_total = jnp.sum(weights, axis=1, keepdims=True)
        probs_low = (weights / row_total).astype(jnp.bfloat16)
        pieces.append(
            jnp.dot(probs_low, value_block[:finish], preferred_element_type=jnp.float32).astype(
                jnp.bfloat16
            )
        )
        row_tops.append(row_top)
        row_totals.append(row_total)
    return (jnp.concatenate(pieces, axis=0), row_tops, row_totals)


def backward_pass(
    query_block,
    key_block,
    value_block,
    grad_block,
    attended_block,
    row_tops,
    row_totals,
    block_rows,
    score_scale,
):
    row_count, head_width = query_block.shape
    grad_key_sum = jnp.zeros((row_count, head_width), jnp.float32)
    grad_value_sum = jnp.zeros((row_count, head_width), jnp.float32)
    query_parts = []
    for block_index in range(row_count // block_rows):
        row_start = block_index * block_rows
        finish = row_start + block_rows
        scores = masked_scores(
            query_block[row_start:finish], key_block[:finish], row_start, score_scale
        )
        probabilities = jnp.exp(scores - row_tops[block_index]) / row_totals[block_index]
        probs_low = probabilities.astype(jnp.bfloat16)
        grad_part = grad_block[row_start:finish]
        grad_prob = jnp.einsum(
            "qd,kd->qk", grad_part, value_block[:finish], preferred_element_type=jnp.float32
        )
        row_delta = jnp.sum(
            grad_part.astype(jnp.float32) * attended_block[row_start:finish].astype(jnp.float32),
            axis=1,
            keepdims=True,
        )
        grad_score = (probabilities * (grad_prob - row_delta)).astype(jnp.bfloat16)
        query_parts.append(
            (
                jnp.dot(grad_score, key_block[:finish], preferred_element_type=jnp.float32)
                * score_scale
            ).astype(jnp.bfloat16)
        )
        key_term = jnp.einsum(
            "qk,qd->kd",
            grad_score,
            query_block[row_start:finish],
            preferred_element_type=jnp.float32,
        )
        value_term = jnp.einsum(
            "qk,qd->kd", probs_low, grad_part, preferred_element_type=jnp.float32
        )
        grad_key_sum = grad_key_sum + jnp.pad(key_term, ((0, row_count - finish), (0, 0)))
        grad_value_sum = grad_value_sum + jnp.pad(value_term, ((0, row_count - finish), (0, 0)))
    grad_query_block = jnp.concatenate(query_parts, axis=0)
    grad_key_block = (grad_key_sum * score_scale).astype(jnp.bfloat16)
    grad_value_block = grad_value_sum.astype(jnp.bfloat16)
    return jnp.stack((grad_query_block, grad_key_block, grad_value_block), axis=1)


def attention_kernel(place_ref, arrived_ref, out_ref, x_ref, y_ref, dk_acc, dv_acc, *, block_rows):
    rows, width = x_ref.shape
    head_width = width // 4
    scale = 1.0 / math.sqrt(head_width)
    order = (
        lax.broadcasted_iota(jnp.int32, (rows, place_ref.shape[1]), 0) == place_ref[...]
    ).astype(jnp.bfloat16)
    x_ref[...] = jnp.dot(order, arrived_ref[...], preferred_element_type=jnp.float32).astype(
        jnp.bfloat16
    )
    dk_acc[...] = jnp.zeros_like(dk_acc)
    dv_acc[...] = jnp.zeros_like(dv_acc)
    for block_index in range(rows // block_rows):
        start = block_index * block_rows
        finish = start + block_rows
        q_part = x_ref[start:finish, 0:head_width]
        g_part = x_ref[start:finish, 3 * head_width : 4 * head_width]
        k_seen = x_ref[0:finish, head_width : 2 * head_width]
        v_seen = x_ref[0:finish, 2 * head_width : 3 * head_width]
        scores = (
            lax.dot_general(q_part, k_seen, (((1,), (1,)), ((), ())), preferred_element_type=jnp.float32)
            * scale
        )
        row_ids = start + lax.broadcasted_iota(jnp.int32, scores.shape, 0)
        col_ids = lax.broadcasted_iota(jnp.int32, scores.shape, 1)
        scores = jnp.where(col_ids <= row_ids, scores, -jnp.inf)
        row_top = jnp.max(scores, axis=1, keepdims=True)
        weights = jnp.exp(scores - row_top)
        probabilities = weights / jnp.sum(weights, axis=1, keepdims=True)
        probs_low = probabilities.astype(jnp.bfloat16)
        attended = jnp.dot(probs_low, v_seen, preferred_element_type=jnp.float32).astype(jnp.bfloat16)
        y_ref[start:finish, 0:head_width] = attended
        grad_prob = lax.dot_general(
            g_part, v_seen, (((1,), (1,)), ((), ())), preferred_element_type=jnp.float32
        )
        row_delta = jnp.sum(
            g_part.astype(jnp.float32) * attended.astype(jnp.float32), axis=1, keepdims=True
        )
        grad_score = (probabilities * (grad_prob - row_delta)).astype(jnp.bfloat16)
        y_ref[start:finish, head_width : 2 * head_width] = (
            jnp.dot(grad_score, k_seen, preferred_element_type=jnp.float32) * scale
        ).astype(jnp.bfloat16)
        dk_acc[0:finish, :] += lax.dot_general(
            grad_score, q_part, (((0,), (0,)), ((), ())), preferred_element_type=jnp.float32
        )
        dv_acc[0:finish, :] += lax.dot_general(
            probs_low, g_part, (((0,), (0,)), ((), ())), preferred_element_type=jnp.float32
        )
    y_ref[:, 2 * head_width : 3 * head_width] = (dk_acc[...] * scale).astype(jnp.bfloat16)
    y_ref[:, 3 * head_width : 4 * head_width] = dv_acc[...].astype(jnp.bfloat16)
    result = lax.dot_general(
        order, y_ref[...], (((0,), (0,)), ((), ())), preferred_element_type=jnp.float32
    )
    for member in range(4):
        out_ref[pl.ds(member, place_ref.shape[1], stride=4), :] = result[
            :, member * head_width : (member + 1) * head_width
        ]


def fused_attention(flat_place, arrived_flat, cluster_len, block_rows=256):
    slots, width = arrived_flat.shape
    return pl.pallas_call(
        functools.partial(attention_kernel, block_rows=block_rows),
        out_shape=jax.ShapeDtypeStruct((slots * 4, width // 4), jnp.float32),
        scratch_shapes=[
            pltpu.VMEM((cluster_len, width), jnp.bfloat16),
            pltpu.VMEM((cluster_len, width), jnp.bfloat16),
            pltpu.VMEM((cluster_len, width // 4), jnp.float32),
            pltpu.VMEM((cluster_len, width // 4), jnp.float32),
        ],
    )(flat_place.reshape(1, slots), arrived_flat)


def shards(query_rows, key_rows, value_rows, grad_rows, assignment, position):
    sub_rows, head_count, head_width = query_rows.shape
    clusters = lax.axis_size("seq")
    cluster_len = sub_rows * lax.axis_size("head")
    capacity = 3 * sub_rows // (2 * clusters)
    slot_count = clusters * capacity
    devices = clusters * head_count
    order = ("head", "seq")
    local_slot = cluster_slots(assignment, clusters, capacity)
    slot_ids = jnp.arange(slot_count, dtype=jnp.int32)
    hits = slot_ids[None, :, None] == local_slot.T[:, None, :]
    hits_low = hits.astype(jnp.bfloat16)
    stacked = jnp.stack((query_rows, key_rows, value_rows, grad_rows), axis=2)
    packed = jnp.einsum(
        "hsr,rhf->hsf",
        hits_low,
        stacked.reshape(sub_rows, head_count, 4 * head_width),
        preferred_element_type=jnp.float32,
    ).astype(jnp.bfloat16)
    places = jnp.where(
        jnp.any(hits, axis=2),
        jnp.sum(jnp.where(hits, position.T[:, None, :], 0), axis=2),
        cluster_len,
    ).reshape(devices, capacity)
    coded = jnp.concatenate((places // 32, places % 32), axis=1).astype(jnp.bfloat16)
    coded = jnp.pad(coded, ((0, 0), (0, 2 * head_width - 2 * capacity))).reshape(
        devices, 1, 2, head_width
    )
    payload = jnp.concatenate(
        (packed.reshape(devices, capacity * 2, 2, head_width), coded), axis=1
    )
    rows = 2 * payload.shape[1]
    arrived = lax.all_to_all(payload, order, 0, 0, tiled=True).reshape(devices, rows, head_width)
    arrived_data = arrived[:, : capacity * 4].reshape(devices * capacity, 4 * head_width)
    arrived_code = arrived[:, capacity * 4].astype(jnp.float32)
    flat_place = (
        arrived_code[:, :capacity] * 32.0 + arrived_code[:, capacity : 2 * capacity]
    ).astype(jnp.int32).reshape(-1)
    all_slots = (
        fused_attention(flat_place, arrived_data, cluster_len)
        .astype(jnp.bfloat16)
        .reshape(devices, capacity, 4, head_width)
    )
    returned = lax.all_to_all(all_slots, order, 0, 0, tiled=True).reshape(
        devices * capacity, 4 * head_width
    )
    back_target = (jnp.arange(head_count, dtype=jnp.int32)[None, :] * slot_count + local_slot).reshape(-1)
    back_hits = (
        jnp.arange(devices * capacity, dtype=jnp.int32)[None, :] == back_target[:, None]
    ).astype(jnp.bfloat16)
    everything = jnp.dot(back_hits, returned, preferred_element_type=jnp.float32)
    return tuple(
        everything[:, member * head_width : (member + 1) * head_width]
        .astype(jnp.bfloat16)
        .reshape(sub_rows, head_count, head_width)
        for member in range(4)
    )


def solution(mesh):
    return jax.shard_map(
        shards,
        mesh=mesh,
        in_specs=(
            P(("seq", "head"), None, None),
            P(("seq", "head"), None, None),
            P(("seq", "head"), None, None),
            P(("seq", "head"), None, None),
            P(("seq", "head"), None),
            P(("seq", "head"), None),
        ),
        out_specs=(
            P(("seq", "head"), None, None),
            P(("seq", "head"), None, None),
            P(("seq", "head"), None, None),
            P(("seq", "head"), None, None),
        ),
        check_vma=False,
    )
```
